128 devices in a mesh: row: 16 (over z, y), col: 8 (over x, core).
Axes of the slice: x: 4, y: 4, z: 4, core: 2. Of those that a mesh axis runs over, the one named last changes fastest.
Arguments:
- holograms: float32 [2, 8192, 8192], P(None, 'row', 'col'), may hold values from -6 to 6
- sideband_centre: int32 [2, 2], replicated, may hold values from 1024 to 4095
- strip_owner: int32 [128], replicated, may hold values from 0 to 127, as said below
Outputs:
- slm_pattern: float32 [2, 2, 12288, 4096], P(None, None, ('row', 'col'))
The draws below stay inside these ranges and needn't reach their ends.
Inputs may be any that keep to these rules, and one draw needn't show every extreme that they name: `strip_owner`: every device drives at most 3 strips, and in every draw some device drives exactly 3; some drive none.
All inputs are finite; a program needn't handle non-finite values.
Results may differ from the reference program's by a relative error of at most 0.0003.
Values sent between devices are 32-bit elements; how exact they have to be, the bound alone decides.
No kernel may reach another device: no remote copies, remote signals or barrier semaphores. Data moves between devices by JAX's collectives and lax.ppermute only.
A program may use at most 128 MiB of HBM per device.

```python
import jax
import jax.numpy as jnp
from jax import lax

H = 8192
S = 2048
P_SIZE = 4096
K = 2
MOST = 3
STRIPS = 128


def draw_strip_owner(key, part):
    devices = STRIPS
    groups = devices // 4
    patterns = jnp.array([[3, 1, 0, 0], [2, 1, 1, 0], [1, 1, 1, 1], [2, 2, 0, 0]], jnp.int32)
    first_key, second_key, third_key = jax.random.split(key, 3)
    chosen = jax.random.randint(first_key, (groups,), 0, 4)
    chosen = chosen.at[0].set(0)
    counts = patterns[chosen].reshape(-1)
    order = jax.random.permutation(second_key, devices)
    counts = counts[order]
    owners = jnp.repeat(jnp.arange(devices, dtype=jnp.int32), counts, total_repeat_length=devices)
    mixing = jax.random.permutation(third_key, devices)
    return owners[mixing].astype(jnp.int32)


def place_ends(drawn, stream_key, low, top_value):
    spot = [jax.random.randint(jax.random.fold_in(stream_key, axis), (), 0, length) for axis, length in enumerate(drawn.shape)]
    widest = drawn.shape.index(max(drawn.shape))
    beside = spot[:widest] + [(spot[widest] + 1) % drawn.shape[widest]] + spot[widest + 1:]
    return drawn.at[tuple(spot)].set(low).at[tuple(beside)].set(top_value)


def level_of(rng, dims, shards, low, top_value):
    def one(position, shards_of):
        heights = jax.random.uniform(jax.random.fold_in(jax.random.fold_in(rng, 6), position), (shards_of,), jnp.float32, low / len(shards), top_value / len(shards))
        return jnp.repeat(jnp.exp(heights), dims[position] // shards_of).reshape((-1,) + (1,) * (len(dims) - position - 1))

    factor_of = one(*shards[0])
    for cut in shards[1:]:
        factor_of = factor_of * one(*cut)
    return factor_of


def gaussian(key, shape, deviation, limit, shards=(), held_as=jnp.bfloat16):
    drawn = deviation * jax.random.normal(key, shape, jnp.float32)
    if shards:
        drawn = drawn * level_of(key, shape, shards, -0.22, 0.18)
    return jnp.clip(drawn, -limit, limit).astype(held_as)


def setup_inputs(seed: int = 0) -> dict:
    splits = jax.random.split(jax.random.key(seed), 4)
    holograms = gaussian(splits[0], (K, H, H), 1.0, 6.0, ((1, 16), (2, 8)), jnp.float32)
    sideband_centre = place_ends(jax.random.randint(splits[1], (K, 2), S // 2, H // 2), jax.random.fold_in(splits[1], 1), S // 2, (H // 2) - 1).astype(jnp.int32)
    strip_owner = draw_strip_owner(jax.random.fold_in(splits[3], 71), 0)
    return {"holograms": holograms, "sideband_centre": sideband_centre, "strip_owner": strip_owner}


headroom = 1.25
softness = 0.01
epsilon = 1e-06

def encode(field_real, field_imag, peak):
    scale = headroom * peak + epsilon
    unit_real = field_real / scale
    unit_imag = field_imag / scale
    square = unit_real * unit_real + unit_imag * unit_imag
    height = jnp.sqrt(1.0 - square)
    spread = jnp.sqrt(square + softness)
    phase_real = unit_real / spread
    phase_imag = unit_imag / spread
    plus_real = unit_real - phase_imag * height
    plus_imag = unit_imag + phase_real * height
    minus_real = unit_real + phase_imag * height
    minus_imag = unit_imag - phase_real * height
    return (plus_real, plus_imag, minus_real, minus_imag)

def slot_sources(strip_owner):
    strips = strip_owner.shape[0]
    strip_ids = jnp.arange(strips, dtype=jnp.int32)
    same = strip_owner[:, None] == strip_owner[None, :]
    before = strip_ids[None, :] < strip_ids[:, None]
    rank = lax.optimization_barrier(jnp.sum((same & before).astype(jnp.int32), axis=1))
    slot_of = strip_owner * MOST + rank
    slot_ids = jnp.arange(strips * MOST, dtype=jnp.int32)
    match = slot_of[None, :] == slot_ids[:, None]
    source = lax.optimization_barrier(jnp.sum(jnp.where(match, strip_ids[None, :], 0), axis=1)).astype(jnp.int32)
    filled = jnp.any(match, axis=1).astype(jnp.float32)
    return (source, filled)

def reference(holograms, sideband_centre, strip_owner):
    strips = strip_owner.shape[0]
    strip_rows = P_SIZE // strips
    source, filled = slot_sources(strip_owner)
    half = S // 2
    offsets = jnp.arange(S, dtype=jnp.int32) - half
    place = offsets % P_SIZE
    row_number = (source[:, None] * strip_rows + jnp.arange(strip_rows, dtype=jnp.int32)[None, :]).reshape(-1)
    keep = jnp.repeat(filled, strip_rows)
    even = (row_number[:, None] + jnp.arange(P_SIZE, dtype=jnp.int32)[None, :]) % 2 == 0

    def one_frame(inputs):
        image, centre = inputs
        spectrum = jnp.fft.fft2(image)
        rows_u = (centre[0] + offsets) % H
        cols_v = (centre[1] + offsets) % H
        band = spectrum[rows_u][:, cols_v]
        padded = jnp.zeros((P_SIZE, P_SIZE), band.dtype).at[place[:, None], place[None, :]].set(band)
        field = jnp.fft.ifft2(padded) * (P_SIZE * P_SIZE)
        field_real = jnp.real(field)
        field_imag = jnp.imag(field)
        peak = jnp.max(jnp.sqrt(field_real * field_real + field_imag * field_imag))
        pick_real = field_real[row_number]
        pick_imag = field_imag[row_number]
        plus_real, plus_imag, minus_real, minus_imag = encode(pick_real, pick_imag, peak)
        out_real = jnp.where(even, plus_real, minus_real) * keep[:, None]
        out_imag = jnp.where(even, plus_imag, minus_imag) * keep[:, None]
        return jnp.stack([out_real, out_imag])
    return lax.map(one_frame, (holograms, sideband_centre))
```

```python
import math

import jax
import jax.numpy as jnp
from jax import lax
from jax.sharding import PartitionSpec as P

H = 8192
S = 2048
P_SIZE = 4096
MOST = 3


two_pi = 2.0 * math.pi
radix = 128
headroom = 1.25
softness = 0.01
epsilon = 1e-06


def contract(form, left, right):
    return jnp.einsum(
        form, left, right, precision=lax.Precision.HIGHEST, preferred_element_type=jnp.float32
    )


def make_tables(frequency, in_len, length, offset, sign):
    accum = length // radix
    blocks = in_len // radix
    first = frequency[:, :accum] % accum
    inner_index = first[:, :, None] * jnp.arange(blocks, dtype=jnp.int32)[None, None, :] % accum
    inner_angle = sign * two_pi / accum * inner_index.astype(jnp.float32)
    column = (jnp.arange(radix, dtype=jnp.int32) + offset) % length
    outer_index = frequency[:, :, None] * column[None, None, :] % length
    outer_angle = sign * two_pi / length * outer_index.astype(jnp.float32)
    shape_four = (frequency.shape[0], frequency.shape[1] // accum, accum, radix)
    return (
        jnp.cos(inner_angle),
        jnp.sin(inner_angle),
        jnp.cos(outer_angle).reshape(shape_four),
        jnp.sin(outer_angle).reshape(shape_four),
    )


def transform(real_part, imag_part, tables):
    inner_cos, inner_sin, outer_cos, outer_sin = tables
    batch, rows, width = real_part.shape
    blocks = width // radix
    real_four = real_part.reshape(batch, rows, blocks, radix)
    mid_real = contract("kpa,krab->krpb", inner_cos, real_four)
    mid_imag = contract("kpa,krab->krpb", inner_sin, real_four)
    if imag_part is not None:
        imag_four = imag_part.reshape(batch, rows, blocks, radix)
        mid_real = mid_real - contract("kpa,krab->krpb", inner_sin, imag_four)
        mid_imag = mid_imag + contract("kpa,krab->krpb", inner_cos, imag_four)
    out_real = contract("kqpb,krpb->krqp", outer_cos, mid_real) - contract(
        "kqpb,krpb->krqp", outer_sin, mid_imag
    )
    out_imag = contract("kqpb,krpb->krqp", outer_cos, mid_imag) + contract(
        "kqpb,krpb->krqp", outer_sin, mid_real
    )
    count = outer_cos.shape[1] * outer_cos.shape[2]
    return (out_real.reshape(batch, rows, count), out_imag.reshape(batch, rows, count))


def encode(field_real, field_imag, peak):
    scale = headroom * peak + epsilon
    unit_real = field_real / scale
    unit_imag = field_imag / scale
    square = unit_real * unit_real + unit_imag * unit_imag
    height = jnp.sqrt(1.0 - square)
    spread = jnp.sqrt(square + softness)
    phase_real = unit_real / spread
    phase_imag = unit_imag / spread
    plus_real = unit_real - phase_imag * height
    plus_imag = unit_imag + phase_real * height
    minus_real = unit_real + phase_imag * height
    minus_imag = unit_imag - phase_real * height
    return (plus_real, plus_imag, minus_real, minus_imag)


def body(holograms, sideband_centre, strip_owner):
    holo_count = holograms.shape[0]
    row_devices = lax.axis_size("row")
    col_devices = lax.axis_size("col")
    devices = row_devices * col_devices
    half = S // 2
    offsets = jnp.arange(S, dtype=jnp.int32) - half
    along_u = (sideband_centre[:, 0:1] + offsets[None, :]) % H
    along_v = (sideband_centre[:, 1:2] + offsets[None, :]) % H
    table_v = make_tables(along_v, H, H, 0, -1.0)
    table_u = make_tables(along_u, H, H, 0, -1.0)
    pixels = lax.optimization_barrier(
        jnp.broadcast_to(jnp.arange(P_SIZE, dtype=jnp.int32)[None, :], (holo_count, P_SIZE))
    )
    table_p = make_tables(pixels, S, P_SIZE, P_SIZE - half, 1.0)
    local_rows = holograms.shape[1]
    local_cols = holograms.shape[2]
    blocks = holograms.reshape(holo_count, col_devices, local_rows // col_devices, local_cols)
    piece = lax.all_to_all(blocks, "col", split_axis=1, concat_axis=3, tiled=True)
    lead, single, count, width = piece.shape
    out_real, out_imag = transform(piece.reshape(lead, count, width), None, table_v)
    spec_real = out_real.reshape(lead, single, count, S)
    spec_imag = out_imag.reshape(lead, single, count, S)
    pencil = spec_real.shape[2]
    share = S // devices
    col_real = jnp.swapaxes(spec_real.reshape(holo_count, pencil, S), 1, 2)
    col_imag = jnp.swapaxes(spec_imag.reshape(holo_count, pencil, S), 1, 2)
    col_both = jnp.stack([col_real, col_imag]).reshape(2, holo_count, devices, share, pencil)
    piece_both = lax.all_to_all(col_both, ("row", "col"), split_axis=2, concat_axis=4, tiled=True)
    piece_real = piece_both[0]
    piece_imag = piece_both[1]
    lead, single, count, width = piece_real.shape
    out_real, out_imag = transform(
        piece_real.reshape(lead, count, width), piece_imag.reshape(lead, count, width), table_u
    )
    side_real = out_real.reshape(lead, single, count, S)
    side_imag = out_imag.reshape(lead, single, count, S)
    lift_real, lift_imag = transform(
        side_real.reshape(holo_count, share, S), side_imag.reshape(holo_count, share, S), table_p
    )
    strips = strip_owner.shape[0]
    strip_rows = P_SIZE // strips
    slot_rows = MOST * strip_rows
    strip_ids = jnp.arange(strips, dtype=jnp.int32)
    same = strip_owner[:, None] == strip_owner[None, :]
    before = strip_ids[None, :] < strip_ids[:, None]
    rank = jnp.sum((same & before).astype(jnp.int32), axis=1)
    slot_of = strip_owner * MOST + rank
    slot_ids = jnp.arange(strips * MOST, dtype=jnp.int32)
    match = slot_of[None, :] == slot_ids[:, None]
    source = jnp.sum(jnp.where(match, strip_ids[None, :], 0), axis=1)
    filled = jnp.any(match, axis=1).astype(jnp.float32)

    def pack(part):
        grouped = part.reshape(holo_count, share, strips, strip_rows)
        picked = jnp.take(grouped, source, axis=2) * filled[None, None, :, None]
        return jnp.transpose(picked.reshape(holo_count, share, strips, slot_rows), (2, 0, 1, 3))

    send_both = jnp.stack([pack(lift_real), pack(lift_imag)], axis=1)
    piece_both = lax.all_to_all(send_both, ("row", "col"), split_axis=0, concat_axis=3, tiled=True)
    piece_real = piece_both[:, 0]
    piece_imag = piece_both[:, 1]
    single, lead, width, count = piece_real.shape
    rows_real = jnp.swapaxes(piece_real.reshape(lead, width, count), 1, 2)
    rows_imag = jnp.swapaxes(piece_imag.reshape(lead, width, count), 1, 2)
    out_real, out_imag = transform(rows_real, rows_imag, table_p)
    field_real = out_real.reshape(single, lead, count, P_SIZE)
    field_imag = out_imag.reshape(single, lead, count, P_SIZE)
    field_real = field_real.reshape(holo_count, slot_rows, P_SIZE)
    field_imag = field_imag.reshape(holo_count, slot_rows, P_SIZE)
    magnitude = jnp.sqrt(field_real * field_real + field_imag * field_imag)
    local_peak = jnp.max(magnitude, axis=(1, 2))
    peak = lax.pmax(lax.pmax(local_peak, "col"), "row")
    plus_real, plus_imag, minus_real, minus_imag = encode(
        field_real, field_imag, peak[:, None, None]
    )
    device_index = lax.axis_index("row") * col_devices + lax.axis_index("col")
    my_source = lax.dynamic_slice_in_dim(source, device_index * MOST, MOST)
    row_number = (
        my_source[:, None] * strip_rows + jnp.arange(strip_rows, dtype=jnp.int32)[None, :]
    ).reshape(slot_rows)
    even = (row_number[:, None] + jnp.arange(P_SIZE, dtype=jnp.int32)[None, :]) % 2 == 0
    out_real = jnp.where(even[None, :, :], plus_real, minus_real)
    out_imag = jnp.where(even[None, :, :], plus_imag, minus_imag)
    return jnp.stack([out_real, out_imag], axis=1)


def solution(mesh):
    placed = (P(None, "row", "col"), P(), P())
    return jax.shard_map(
        body,
        mesh=mesh,
        in_specs=placed,
        out_specs=P(None, None, ("row", "col"), None),
        check_vma=False,
    )
```

```python
import math

import jax
import jax.numpy as jnp
from jax import lax
from jax.sharding import PartitionSpec as P

H = 8192
S = 2048
P_SIZE = 4096
MOST = 3


two_pi = 2.0 * math.pi
radix = 128
headroom = 1.25
softness = 0.01
epsilon = 1e-06


def contract(form, left, right):
    return jnp.einsum(
        form, left, right, precision=lax.Precision.HIGHEST, preferred_element_type=jnp.float32
    )


def make_tables(frequency, in_len, length, offset, sign):
    accum = length // radix
    blocks = in_len // radix
    first = frequency[:, :accum] % accum
    inner_index = first[:, :, None] * jnp.arange(blocks, dtype=jnp.int32)[None, None, :] % accum
    inner_angle = sign * two_pi / accum * inner_index.astype(jnp.float32)
    column = (jnp.arange(radix, dtype=jnp.int32) + offset) % length
    outer_index = frequency[:, :, None] * column[None, None, :] % length
    outer_angle = sign * two_pi / length * outer_index.astype(jnp.float32)
    shape_four = (frequency.shape[0], frequency.shape[1] // accum, accum, radix)
    return lax.optimization_barrier(
        (
            jnp.cos(inner_angle),
            jnp.sin(inner_angle),
            jnp.cos(outer_angle).reshape(shape_four),
            jnp.sin(outer_angle).reshape(shape_four),
        )
    )


def transform(real_part, imag_part, tables):
    inner_cos, inner_sin, outer_cos, outer_sin = tables
    batch, rows, width = real_part.shape
    blocks = width // radix
    real_four = real_part.reshape(batch, rows, blocks, radix)
    mid_real = contract("kpa,krab->krpb", inner_cos, real_four)
    mid_imag = contract("kpa,krab->krpb", inner_sin, real_four)
    if imag_part is not None:
        imag_four = imag_part.reshape(batch, rows, blocks, radix)
        mid_real = mid_real - contract("kpa,krab->krpb", inner_sin, imag_four)
        mid_imag = mid_imag + contract("kpa,krab->krpb", inner_cos, imag_four)
    out_real = contract("kqpb,krpb->krqp", outer_cos, mid_real) - contract(
        "kqpb,krpb->krqp", outer_sin, mid_imag
    )
    out_imag = contract("kqpb,krpb->krqp", outer_cos, mid_imag) + contract(
        "kqpb,krpb->krqp", outer_sin, mid_real
    )
    count = outer_cos.shape[1] * outer_cos.shape[2]
    return (out_real.reshape(batch, rows, count), out_imag.reshape(batch, rows, count))


def encode(field_real, field_imag, peak):
    scale = headroom * peak + epsilon
    unit_real = field_real / scale
    unit_imag = field_imag / scale
    square = unit_real * unit_real + unit_imag * unit_imag
    height = jnp.sqrt(1.0 - square)
    spread = jnp.sqrt(square + softness)
    phase_real = unit_real / spread
    phase_imag = unit_imag / spread
    plus_real = unit_real - phase_imag * height
    plus_imag = unit_imag + phase_real * height
    minus_real = unit_real + phase_imag * height
    minus_imag = unit_imag - phase_real * height
    return (plus_real, plus_imag, minus_real, minus_imag)


def body(holograms, sideband_centre, strip_owner):
    holo_count = holograms.shape[0]
    row_devices = lax.axis_size("row")
    col_devices = lax.axis_size("col")
    devices = row_devices * col_devices
    half = S // 2
    offsets = jnp.arange(S, dtype=jnp.int32) - half
    along_u = (sideband_centre[:, 0:1] + offsets[None, :]) % H
    along_v = (sideband_centre[:, 1:2] + offsets[None, :]) % H
    table_v = make_tables(along_v, H, H, 0, -1.0)
    table_u = make_tables(along_u, H, H, 0, -1.0)
    pixels = jnp.broadcast_to(jnp.arange(P_SIZE, dtype=jnp.int32)[None, :], (holo_count, P_SIZE))
    table_p = make_tables(pixels, S, P_SIZE, P_SIZE - half, 1.0)
    local_rows = holograms.shape[1]
    local_cols = holograms.shape[2]
    blocks = holograms.reshape(holo_count, col_devices, local_rows // col_devices, local_cols)
    piece = lax.all_to_all(blocks, "col", split_axis=1, concat_axis=3, tiled=True)
    lead, single, count, width = piece.shape
    out_real, out_imag = transform(piece.reshape(lead, count, width), None, table_v)
    spec_real = out_real.reshape(lead, single, count, S)
    spec_imag = out_imag.reshape(lead, single, count, S)
    pencil = spec_real.shape[2]
    share = S // devices
    col_real = jnp.swapaxes(spec_real.reshape(holo_count, pencil, S), 1, 2)
    col_imag = jnp.swapaxes(spec_imag.reshape(holo_count, pencil, S), 1, 2)
    piece_real = lax.all_to_all(
        col_real.reshape(holo_count, devices, share, pencil),
        ("row", "col"),
        split_axis=1,
        concat_axis=3,
        tiled=True,
    )
    piece_imag = lax.all_to_all(
        col_imag.reshape(holo_count, devices, share, pencil),
        ("row", "col"),
        split_axis=1,
        concat_axis=3,
        tiled=True,
    )
    lead, single, count, width = piece_real.shape
    out_real, out_imag = transform(
        piece_real.reshape(lead, count, width), piece_imag.reshape(lead, count, width), table_u
    )
    side_real = out_real.reshape(lead, single, count, S)
    side_imag = out_imag.reshape(lead, single, count, S)
    lift_real, lift_imag = transform(
        side_real.reshape(holo_count, share, S), side_imag.reshape(holo_count, share, S), table_p
    )
    strips = strip_owner.shape[0]
    strip_rows = P_SIZE // strips
    slot_rows = MOST * strip_rows
    strip_ids = jnp.arange(strips, dtype=jnp.int32)
    same = strip_owner[:, None] == strip_owner[None, :]
    before = strip_ids[None, :] < strip_ids[:, None]
    rank = jnp.sum((same & before).astype(jnp.int32), axis=1)
    slot_of = strip_owner * MOST + rank
    slot_ids = jnp.arange(strips * MOST, dtype=jnp.int32)
    match = slot_of[None, :] == slot_ids[:, None]
    source = jnp.sum(jnp.where(match, strip_ids[None, :], 0), axis=1)
    filled = jnp.any(match, axis=1).astype(jnp.float32)

    def pack(part):
        grouped = part.reshape(holo_count, share, strips, strip_rows)
        picked = jnp.take(grouped, source, axis=2) * filled[None, None, :, None]
        return jnp.transpose(picked.reshape(holo_count, share, strips, slot_rows), (2, 0, 1, 3))

    send_real = pack(lift_real)
    send_imag = pack(lift_imag)
    piece_real = lax.all_to_all(send_real, ("row", "col"), split_axis=0, concat_axis=2, tiled=True)
    piece_imag = lax.all_to_all(send_imag, ("row", "col"), split_axis=0, concat_axis=2, tiled=True)
    single, lead, width, count = piece_real.shape
    rows_real = jnp.swapaxes(piece_real.reshape(lead, width, count), 1, 2)
    rows_imag = jnp.swapaxes(piece_imag.reshape(lead, width, count), 1, 2)
    out_real, out_imag = transform(rows_real, rows_imag, table_p)
    field_real = out_real.reshape(single, lead, count, P_SIZE)
    field_imag = out_imag.reshape(single, lead, count, P_SIZE)
    field_real = field_real.reshape(holo_count, slot_rows, P_SIZE)
    field_imag = field_imag.reshape(holo_count, slot_rows, P_SIZE)
    magnitude = jnp.sqrt(field_real * field_real + field_imag * field_imag)
    local_peak = jnp.max(magnitude, axis=(1, 2))
    peak = lax.pmax(lax.pmax(local_peak, "col"), "row")
    plus_real, plus_imag, minus_real, minus_imag = encode(
        field_real, field_imag, peak[:, None, None]
    )
    device_index = lax.axis_index("row") * col_devices + lax.axis_index("col")
    my_source = lax.dynamic_slice_in_dim(source, device_index * MOST, MOST)
    row_number = (
        my_source[:, None] * strip_rows + jnp.arange(strip_rows, dtype=jnp.int32)[None, :]
    ).reshape(slot_rows)
    even = (row_number[:, None] + jnp.arange(P_SIZE, dtype=jnp.int32)[None, :]) % 2 == 0
    out_real = jnp.where(even[None, :, :], plus_real, minus_real)
    out_imag = jnp.where(even[None, :, :], plus_imag, minus_imag)
    return jnp.stack([out_real, out_imag], axis=1)


def solution(mesh):
    placed = (P(None, "row", "col"), P(), P())
    return jax.shard_map(
        body,
        mesh=mesh,
        in_specs=placed,
        out_specs=P(None, None, ("row", "col"), None),
        check_vma=False,
    )
```

```python
import math

import jax
import jax.numpy as jnp
from jax import lax
from jax.sharding import PartitionSpec as P

H = 8192
S = 2048
P_SIZE = 4096
MOST = 3


two_pi = 2.0 * math.pi
radix = 128
headroom = 1.25
softness = 0.01
epsilon = 1e-06


def contract(form, left, right):
    return jnp.einsum(
        form, left, right, precision=lax.Precision.HIGH, preferred_element_type=jnp.float32
    )


def make_tables(frequency, in_len, length, offset, sign):
    accum = length // radix
    blocks = in_len // radix
    first = frequency[:, :accum] % accum
    inner_index = first[:, :, None] * jnp.arange(blocks, dtype=jnp.int32)[None, None, :] % accum
    inner_angle = sign * two_pi / accum * inner_index.astype(jnp.float32)
    column = (jnp.arange(radix, dtype=jnp.int32) + offset) % length
    outer_index = frequency[:, :, None] * column[None, None, :] % length
    outer_angle = sign * two_pi / length * outer_index.astype(jnp.float32)
    shape_four = (frequency.shape[0], frequency.shape[1] // accum, accum, radix)
    return lax.optimization_barrier(
        (
            jnp.cos(inner_angle),
            jnp.sin(inner_angle),
            jnp.cos(outer_angle).reshape(shape_four),
            jnp.sin(outer_angle).reshape(shape_four),
        )
    )


def transform(real_part, imag_part, tables):
    inner_cos, inner_sin, outer_cos, outer_sin = tables
    batch, rows, width = real_part.shape
    blocks = width // radix
    real_four = real_part.reshape(batch, rows, blocks, radix)
    mid_real = contract("kpa,krab->krpb", inner_cos, real_four)
    mid_imag = contract("kpa,krab->krpb", inner_sin, real_four)
    if imag_part is not None:
        imag_four = imag_part.reshape(batch, rows, blocks, radix)
        mid_real = mid_real - contract("kpa,krab->krpb", inner_sin, imag_four)
        mid_imag = mid_imag + contract("kpa,krab->krpb", inner_cos, imag_four)
    out_real = contract("kqpb,krpb->krqp", outer_cos, mid_real) - contract(
        "kqpb,krpb->krqp", outer_sin, mid_imag
    )
    out_imag = contract("kqpb,krpb->krqp", outer_cos, mid_imag) + contract(
        "kqpb,krpb->krqp", outer_sin, mid_real
    )
    count = outer_cos.shape[1] * outer_cos.shape[2]
    return (out_real.reshape(batch, rows, count), out_imag.reshape(batch, rows, count))


def encode(field_real, field_imag, peak):
    scale = headroom * peak + epsilon
    unit_real = field_real / scale
    unit_imag = field_imag / scale
    square = unit_real * unit_real + unit_imag * unit_imag
    height = jnp.sqrt(1.0 - square)
    spread = jnp.sqrt(square + softness)
    phase_real = unit_real / spread
    phase_imag = unit_imag / spread
    plus_real = unit_real - phase_imag * height
    plus_imag = unit_imag + phase_real * height
    minus_real = unit_real + phase_imag * height
    minus_imag = unit_imag - phase_real * height
    return (plus_real, plus_imag, minus_real, minus_imag)


def body(holograms, sideband_centre, strip_owner):
    holo_count = holograms.shape[0]
    row_devices = lax.axis_size("row")
    col_devices = lax.axis_size("col")
    devices = row_devices * col_devices
    half = S // 2
    offsets = jnp.arange(S, dtype=jnp.int32) - half
    along_u = (sideband_centre[:, 0:1] + offsets[None, :]) % H
    along_v = (sideband_centre[:, 1:2] + offsets[None, :]) % H
    table_v = make_tables(along_v, H, H, 0, -1.0)
    table_u = make_tables(along_u, H, H, 0, -1.0)
    pixels = jnp.broadcast_to(jnp.arange(P_SIZE, dtype=jnp.int32)[None, :], (holo_count, P_SIZE))
    table_p = make_tables(pixels, S, P_SIZE, P_SIZE - half, 1.0)
    local_rows = holograms.shape[1]
    local_cols = holograms.shape[2]
    blocks = holograms.reshape(holo_count, col_devices, local_rows // col_devices, local_cols)
    piece = lax.all_to_all(blocks, "col", split_axis=1, concat_axis=3, tiled=True)
    lead, single, count, width = piece.shape
    out_real, out_imag = transform(piece.reshape(lead, count, width), None, table_v)
    spec_real = out_real.reshape(lead, single, count, S)
    spec_imag = out_imag.reshape(lead, single, count, S)
    pencil = spec_real.shape[2]
    share = S // devices
    col_real = jnp.swapaxes(spec_real.reshape(holo_count, pencil, S), 1, 2)
    col_imag = jnp.swapaxes(spec_imag.reshape(holo_count, pencil, S), 1, 2)
    piece_real = lax.all_to_all(
        col_real.reshape(holo_count, devices, share, pencil),
        ("row", "col"),
        split_axis=1,
        concat_axis=3,
        tiled=True,
    )
    piece_imag = lax.all_to_all(
        col_imag.reshape(holo_count, devices, share, pencil),
        ("row", "col"),
        split_axis=1,
        concat_axis=3,
        tiled=True,
    )
    lead, single, count, width = piece_real.shape
    out_real, out_imag = transform(
        piece_real.reshape(lead, count, width), piece_imag.reshape(lead, count, width), table_u
    )
    side_real = out_real.reshape(lead, single, count, S)
    side_imag = out_imag.reshape(lead, single, count, S)
    lift_real, lift_imag = transform(
        side_real.reshape(holo_count, share, S), side_imag.reshape(holo_count, share, S), table_p
    )
    strips = strip_owner.shape[0]
    strip_rows = P_SIZE // strips
    slot_rows = MOST * strip_rows
    strip_ids = jnp.arange(strips, dtype=jnp.int32)
    same = strip_owner[:, None] == strip_owner[None, :]
    before = strip_ids[None, :] < strip_ids[:, None]
    rank = jnp.sum((same & before).astype(jnp.int32), axis=1)
    slot_of = strip_owner * MOST + rank
    slot_ids = jnp.arange(strips * MOST, dtype=jnp.int32)
    match = slot_of[None, :] == slot_ids[:, None]
    source = jnp.sum(jnp.where(match, strip_ids[None, :], 0), axis=1)
    filled = jnp.any(match, axis=1).astype(jnp.float32)

    def pack(part):
        grouped = part.reshape(holo_count, share, strips, strip_rows)
        picked = jnp.take(grouped, source, axis=2) * filled[None, None, :, None]
        return jnp.transpose(picked.reshape(holo_count, share, strips, slot_rows), (2, 0, 1, 3))

    send_real = pack(lift_real)
    send_imag = pack(lift_imag)
    piece_real = lax.all_to_all(send_real, ("row", "col"), split_axis=0, concat_axis=2, tiled=True)
    piece_imag = lax.all_to_all(send_imag, ("row", "col"), split_axis=0, concat_axis=2, tiled=True)
    single, lead, width, count = piece_real.shape
    rows_real = jnp.swapaxes(piece_real.reshape(lead, width, count), 1, 2)
    rows_imag = jnp.swapaxes(piece_imag.reshape(lead, width, count), 1, 2)
    out_real, out_imag = transform(rows_real, rows_imag, table_p)
    field_real = out_real.reshape(single, lead, count, P_SIZE)
    field_imag = out_imag.reshape(single, lead, count, P_SIZE)
    field_real = field_real.reshape(holo_count, slot_rows, P_SIZE)
    field_imag = field_imag.reshape(holo_count, slot_rows, P_SIZE)
    magnitude = jnp.sqrt(field_real * field_real + field_imag * field_imag)
    local_peak = jnp.max(magnitude, axis=(1, 2))
    peak = lax.pmax(lax.pmax(local_peak, "col"), "row")
    plus_real, plus_imag, minus_real, minus_imag = encode(
        field_real, field_imag, peak[:, None, None]
    )
    device_index = lax.axis_index("row") * col_devices + lax.axis_index("col")
    my_source = lax.dynamic_slice_in_dim(source, device_index * MOST, MOST)
    row_number = (
        my_source[:, None] * strip_rows + jnp.arange(strip_rows, dtype=jnp.int32)[None, :]
    ).reshape(slot_rows)
    even = (row_number[:, None] + jnp.arange(P_SIZE, dtype=jnp.int32)[None, :]) % 2 == 0
    out_real = jnp.where(even[None, :, :], plus_real, minus_real)
    out_imag = jnp.where(even[None, :, :], plus_imag, minus_imag)
    return jnp.stack([out_real, out_imag], axis=1)


def solution(mesh):
    placed = (P(None, "row", "col"), P(), P())
    return jax.shard_map(
        body,
        mesh=mesh,
        in_specs=placed,
        out_specs=P(None, None, ("row", "col"), None),
        check_vma=False,
    )
```

```python
import math

import jax
import jax.numpy as jnp
from jax import lax
from jax.sharding import PartitionSpec as P

H = 8192
S = 2048
P_SIZE = 4096
MOST = 3


two_pi = 2.0 * math.pi
radix = 128
headroom = 1.25
softness = 0.01
epsilon = 1e-06


def contract(form, left, right):
    return jnp.einsum(
        form, left, right, precision=lax.Precision.HIGH, preferred_element_type=jnp.float32
    )


def make_tables(frequency, in_len, length, offset, sign):
    accum = length // radix
    blocks = in_len // radix
    first = frequency[:, :accum] % accum
    inner_index = first[:, :, None] * jnp.arange(blocks, dtype=jnp.int32)[None, None, :] % accum
    inner_angle = sign * two_pi / accum * inner_index.astype(jnp.float32)
    column = (jnp.arange(radix, dtype=jnp.int32) + offset) % length
    outer_index = frequency[:, :, None] * column[None, None, :] % length
    outer_angle = sign * two_pi / length * outer_index.astype(jnp.float32)
    shape_four = (frequency.shape[0], frequency.shape[1] // accum, accum, radix)
    return lax.optimization_barrier(
        (
            jnp.cos(inner_angle),
            jnp.sin(inner_angle),
            jnp.cos(outer_angle).reshape(shape_four),
            jnp.sin(outer_angle).reshape(shape_four),
        )
    )


def transform(real_part, imag_part, tables):
    inner_cos, inner_sin, outer_cos, outer_sin = tables
    batch, rows, width = real_part.shape
    blocks = width // radix
    real_four = real_part.reshape(batch, rows, blocks, radix)
    mid_real = contract("kpa,krab->krpb", inner_cos, real_four)
    mid_imag = contract("kpa,krab->krpb", inner_sin, real_four)
    if imag_part is not None:
        imag_four = imag_part.reshape(batch, rows, blocks, radix)
        mid_real = mid_real - contract("kpa,krab->krpb", inner_sin, imag_four)
        mid_imag = mid_imag + contract("kpa,krab->krpb", inner_cos, imag_four)
    out_real = contract("kqpb,krpb->krqp", outer_cos, mid_real) - contract(
        "kqpb,krpb->krqp", outer_sin, mid_imag
    )
    out_imag = contract("kqpb,krpb->krqp", outer_cos, mid_imag) + contract(
        "kqpb,krpb->krqp", outer_sin, mid_real
    )
    count = outer_cos.shape[1] * outer_cos.shape[2]
    return (out_real.reshape(batch, rows, count), out_imag.reshape(batch, rows, count))


def encode(field_real, field_imag, peak):
    scale = headroom * peak + epsilon
    unit_real = field_real / scale
    unit_imag = field_imag / scale
    square = unit_real * unit_real + unit_imag * unit_imag
    height = jnp.sqrt(1.0 - square)
    spread = jnp.sqrt(square + softness)
    phase_real = unit_real / spread
    phase_imag = unit_imag / spread
    plus_real = unit_real - phase_imag * height
    plus_imag = unit_imag + phase_real * height
    minus_real = unit_real + phase_imag * height
    minus_imag = unit_imag - phase_real * height
    return (plus_real, plus_imag, minus_real, minus_imag)


def body(holograms, sideband_centre, strip_owner):
    holo_count = holograms.shape[0]
    row_devices = lax.axis_size("row")
    col_devices = lax.axis_size("col")
    devices = row_devices * col_devices
    half = S // 2
    offsets = jnp.arange(S, dtype=jnp.int32) - half
    along_u = (sideband_centre[:, 0:1] + offsets[None, :]) % H
    along_v = (sideband_centre[:, 1:2] + offsets[None, :]) % H
    table_v = make_tables(along_v, H, H, 0, -1.0)
    table_u = make_tables(along_u, H, H, 0, -1.0)
    pixels = jnp.broadcast_to(jnp.arange(P_SIZE, dtype=jnp.int32)[None, :], (holo_count, P_SIZE))
    table_p = make_tables(pixels, S, P_SIZE, P_SIZE - half, 1.0)
    local_rows = holograms.shape[1]
    local_cols = holograms.shape[2]
    blocks = holograms.reshape(holo_count, col_devices, local_rows // col_devices, local_cols)
    piece = lax.all_to_all(blocks, "col", split_axis=1, concat_axis=3, tiled=True)
    lead, single, count, width = piece.shape
    out_real, out_imag = transform(piece.reshape(lead, count, width), None, table_v)
    spec_real = out_real.reshape(lead, single, count, S)
    spec_imag = out_imag.reshape(lead, single, count, S)
    pencil = spec_real.shape[2]
    share = S // devices
    col_real = jnp.swapaxes(spec_real.reshape(holo_count, pencil, S), 1, 2)
    col_imag = jnp.swapaxes(spec_imag.reshape(holo_count, pencil, S), 1, 2)
    piece_real = lax.all_to_all(
        col_real.reshape(holo_count, devices, share, pencil),
        ("row", "col"),
        split_axis=1,
        concat_axis=3,
        tiled=True,
    )
    piece_imag = lax.all_to_all(
        col_imag.reshape(holo_count, devices, share, pencil),
        ("row", "col"),
        split_axis=1,
        concat_axis=3,
        tiled=True,
    )
    lead, single, count, width = piece_real.shape
    out_real, out_imag = transform(
        piece_real.reshape(lead, count, width), piece_imag.reshape(lead, count, width), table_u
    )
    side_real = out_real.reshape(lead, single, count, S)
    side_imag = out_imag.reshape(lead, single, count, S)
    lift_real, lift_imag = transform(
        side_real.reshape(holo_count, share, S), side_imag.reshape(holo_count, share, S), table_p
    )
    strips = strip_owner.shape[0]
    strip_rows = P_SIZE // strips
    slot_rows = MOST * strip_rows
    strip_ids = jnp.arange(strips, dtype=jnp.int32)
    same = strip_owner[:, None] == strip_owner[None, :]
    before = strip_ids[None, :] < strip_ids[:, None]
    rank = jnp.sum((same & before).astype(jnp.int32), axis=1)
    slot_of = strip_owner * MOST + rank
    slot_ids = jnp.arange(strips * MOST, dtype=jnp.int32)
    match = slot_of[None, :] == slot_ids[:, None]
    source = jnp.sum(jnp.where(match, strip_ids[None, :], 0), axis=1)
    filled = jnp.any(match, axis=1).astype(jnp.float32)

    def pack(part):
        grouped = part.reshape(holo_count, share, strips, strip_rows)
        picked = jnp.take(grouped, source, axis=2) * filled[None, None, :, None]
        return jnp.transpose(picked.reshape(holo_count, share, strips, slot_rows), (2, 0, 1, 3))

    send_real = pack(lift_real)
    send_imag = pack(lift_imag)
    piece_real = lax.all_to_all(send_real, ("row", "col"), split_axis=0, concat_axis=2, tiled=True)
    piece_imag = lax.all_to_all(send_imag, ("row", "col"), split_axis=0, concat_axis=2, tiled=True)
    single, lead, width, count = piece_real.shape
    rows_real = jnp.swapaxes(piece_real.reshape(lead, width, count), 1, 2)
    rows_imag = jnp.swapaxes(piece_imag.reshape(lead, width, count), 1, 2)
    out_real, out_imag = transform(rows_real, rows_imag, table_p)
    field_real = out_real.reshape(single, lead, count, P_SIZE)
    field_imag = out_imag.reshape(single, lead, count, P_SIZE)
    field_real = field_real.reshape(holo_count, slot_rows, P_SIZE)
    field_imag = field_imag.reshape(holo_count, slot_rows, P_SIZE)
    magnitude = jnp.sqrt(field_real * field_real + field_imag * field_imag)
    local_peak = jnp.max(magnitude, axis=(1, 2))
    every = jnp.broadcast_to(local_peak[None, :], (devices, holo_count))
    peak = jnp.max(lax.all_to_all(every, ("row", "col"), 0, 0, tiled=True), axis=0)
    plus_real, plus_imag, minus_real, minus_imag = encode(
        field_real, field_imag, peak[:, None, None]
    )
    device_index = lax.axis_index("row") * col_devices + lax.axis_index("col")
    my_source = lax.dynamic_slice_in_dim(source, device_index * MOST, MOST)
    row_number = (
        my_source[:, None] * strip_rows + jnp.arange(strip_rows, dtype=jnp.int32)[None, :]
    ).reshape(slot_rows)
    even = (row_number[:, None] + jnp.arange(P_SIZE, dtype=jnp.int32)[None, :]) % 2 == 0
    out_real = jnp.where(even[None, :, :], plus_real, minus_real)
    out_imag = jnp.where(even[None, :, :], plus_imag, minus_imag)
    return jnp.stack([out_real, out_imag], axis=1)


def solution(mesh):
    placed = (P(None, "row", "col"), P(), P())
    return jax.shard_map(
        body,
        mesh=mesh,
        in_specs=placed,
        out_specs=P(None, None, ("row", "col"), None),
        check_vma=False,
    )
```

```python
import math

import jax
import jax.numpy as jnp
from jax import lax
from jax.sharding import PartitionSpec as P

H = 8192
S = 2048
P_SIZE = 4096
MOST = 3


two_pi = 2.0 * math.pi
radix = 128
headroom = 1.25
softness = 0.01
epsilon = 1e-06


def contract(form, left, right):
    return jnp.einsum(
        form, left, right, precision=lax.Precision.HIGH, preferred_element_type=jnp.float32
    )


def make_tables(frequency, in_len, length, offset, sign):
    accum = length // radix
    blocks = in_len // radix
    first = frequency[:, :accum] % accum
    inner_index = first[:, :, None] * jnp.arange(blocks, dtype=jnp.int32)[None, None, :] % accum
    inner_angle = sign * two_pi / accum * inner_index.astype(jnp.float32)
    column = (jnp.arange(radix, dtype=jnp.int32) + offset) % length
    outer_index = frequency[:, :, None] * column[None, None, :] % length
    outer_angle = sign * two_pi / length * outer_index.astype(jnp.float32)
    shape_four = (frequency.shape[0], frequency.shape[1] // accum, accum, radix)
    return lax.optimization_barrier(
        (
            jnp.cos(inner_angle),
            jnp.sin(inner_angle),
            jnp.cos(outer_angle).reshape(shape_four),
            jnp.sin(outer_angle).reshape(shape_four),
        )
    )


def transform(real_part, imag_part, tables):
    inner_cos, inner_sin, outer_cos, outer_sin = tables
    batch, rows, width = real_part.shape
    blocks = width // radix
    real_four = real_part.reshape(batch, rows, blocks, radix)
    mid_real = contract("kpa,krab->krpb", inner_cos, real_four)
    mid_imag = contract("kpa,krab->krpb", inner_sin, real_four)
    if imag_part is not None:
        imag_four = imag_part.reshape(batch, rows, blocks, radix)
        mid_real = mid_real - contract("kpa,krab->krpb", inner_sin, imag_four)
        mid_imag = mid_imag + contract("kpa,krab->krpb", inner_cos, imag_four)
    out_real = contract("kqpb,krpb->krqp", outer_cos, mid_real) - contract(
        "kqpb,krpb->krqp", outer_sin, mid_imag
    )
    out_imag = contract("kqpb,krpb->krqp", outer_cos, mid_imag) + contract(
        "kqpb,krpb->krqp", outer_sin, mid_real
    )
    count = outer_cos.shape[1] * outer_cos.shape[2]
    return (out_real.reshape(batch, rows, count), out_imag.reshape(batch, rows, count))


def encode(field_real, field_imag, peak):
    scale = headroom * peak + epsilon
    unit_real = field_real / scale
    unit_imag = field_imag / scale
    square = unit_real * unit_real + unit_imag * unit_imag
    height = jnp.sqrt(1.0 - square)
    spread = jnp.sqrt(square + softness)
    phase_real = unit_real / spread
    phase_imag = unit_imag / spread
    plus_real = unit_real - phase_imag * height
    plus_imag = unit_imag + phase_real * height
    minus_real = unit_real + phase_imag * height
    minus_imag = unit_imag - phase_real * height
    return (plus_real, plus_imag, minus_real, minus_imag)


def slot_plan(strip_owner):
    strips = strip_owner.shape[0]
    strip_ids = jnp.arange(strips, dtype=jnp.int32)
    same = strip_owner[:, None] == strip_owner[None, :]
    before = strip_ids[None, :] < strip_ids[:, None]
    rank = jnp.sum((same & before).astype(jnp.int32), axis=1)
    slot_of = strip_owner * MOST + rank
    slot_ids = jnp.arange(strips * MOST, dtype=jnp.int32)
    match = slot_of[None, :] == slot_ids[:, None]
    source = jnp.sum(jnp.where(match, strip_ids[None, :], 0), axis=1)
    filled = jnp.any(match, axis=1).astype(jnp.float32)
    return source, filled


def field_rows(holograms, sideband_centre, source, filled, strips):
    holo_count = holograms.shape[0]
    row_devices = lax.axis_size("row")
    col_devices = lax.axis_size("col")
    devices = row_devices * col_devices
    half = S // 2
    offsets = jnp.arange(S, dtype=jnp.int32) - half
    along_u = (sideband_centre[:, 0:1] + offsets[None, :]) % H
    along_v = (sideband_centre[:, 1:2] + offsets[None, :]) % H
    table_v = make_tables(along_v, H, H, 0, -1.0)
    table_u = make_tables(along_u, H, H, 0, -1.0)
    pixels = jnp.broadcast_to(jnp.arange(P_SIZE, dtype=jnp.int32)[None, :], (holo_count, P_SIZE))
    table_p = make_tables(pixels, S, P_SIZE, P_SIZE - half, 1.0)
    local_rows = holograms.shape[1]
    local_cols = holograms.shape[2]
    blocks = holograms.reshape(holo_count, col_devices, local_rows // col_devices, local_cols)
    piece = lax.all_to_all(blocks, "col", split_axis=1, concat_axis=3, tiled=True)
    lead, single, count, width = piece.shape
    out_real, out_imag = transform(piece.reshape(lead, count, width), None, table_v)
    spec_real = out_real.reshape(lead, single, count, S)
    spec_imag = out_imag.reshape(lead, single, count, S)
    pencil = spec_real.shape[2]
    share = S // devices
    col_real = jnp.swapaxes(spec_real.reshape(holo_count, pencil, S), 1, 2)
    col_imag = jnp.swapaxes(spec_imag.reshape(holo_count, pencil, S), 1, 2)
    piece_real = lax.all_to_all(
        col_real.reshape(holo_count, devices, share, pencil),
        ("row", "col"),
        split_axis=1,
        concat_axis=3,
        tiled=True,
    )
    piece_imag = lax.all_to_all(
        col_imag.reshape(holo_count, devices, share, pencil),
        ("row", "col"),
        split_axis=1,
        concat_axis=3,
        tiled=True,
    )
    lead, single, count, width = piece_real.shape
    out_real, out_imag = transform(
        piece_real.reshape(lead, count, width), piece_imag.reshape(lead, count, width), table_u
    )
    side_real = out_real.reshape(lead, single, count, S)
    side_imag = out_imag.reshape(lead, single, count, S)
    lift_real, lift_imag = transform(
        side_real.reshape(holo_count, share, S), side_imag.reshape(holo_count, share, S), table_p
    )
    strip_rows = P_SIZE // strips
    slot_rows = MOST * strip_rows

    def pack(part):
        grouped = part.reshape(holo_count, share, strips, strip_rows)
        picked = jnp.take(grouped, source, axis=2) * filled[None, None, :, None]
        return jnp.transpose(picked.reshape(holo_count, share, strips, slot_rows), (2, 0, 1, 3))

    send_real = pack(lift_real)
    send_imag = pack(lift_imag)
    piece_real = lax.all_to_all(send_real, ("row", "col"), split_axis=0, concat_axis=2, tiled=True)
    piece_imag = lax.all_to_all(send_imag, ("row", "col"), split_axis=0, concat_axis=2, tiled=True)
    single, lead, width, count = piece_real.shape
    rows_real = jnp.swapaxes(piece_real.reshape(lead, width, count), 1, 2)
    rows_imag = jnp.swapaxes(piece_imag.reshape(lead, width, count), 1, 2)
    out_real, out_imag = transform(rows_real, rows_imag, table_p)
    field_real = out_real.reshape(holo_count, slot_rows, P_SIZE)
    field_imag = out_imag.reshape(holo_count, slot_rows, P_SIZE)
    magnitude = jnp.sqrt(field_real * field_real + field_imag * field_imag)
    local_peak = jnp.max(magnitude, axis=(1, 2))
    return field_real, field_imag, local_peak


def body(holograms, sideband_centre, strip_owner):
    holo_count = holograms.shape[0]
    col_devices = lax.axis_size("col")
    devices = lax.axis_size("row") * col_devices
    strips = strip_owner.shape[0]
    strip_rows = P_SIZE // strips
    slot_rows = MOST * strip_rows
    source, filled = slot_plan(strip_owner)
    parts = [
        field_rows(holograms[k : k + 1], sideband_centre[k : k + 1], source, filled, strips)
        for k in range(holo_count)
    ]
    field_real = jnp.concatenate([part[0] for part in parts])
    field_imag = jnp.concatenate([part[1] for part in parts])
    local_peak = jnp.concatenate([part[2] for part in parts])
    every = jnp.broadcast_to(local_peak[None, :], (devices, holo_count))
    peak = jnp.max(lax.all_to_all(every, ("row", "col"), 0, 0, tiled=True), axis=0)
    plus_real, plus_imag, minus_real, minus_imag = encode(
        field_real, field_imag, peak[:, None, None]
    )
    device_index = lax.axis_index("row") * col_devices + lax.axis_index("col")
    my_source = lax.dynamic_slice_in_dim(source, device_index * MOST, MOST)
    row_number = (
        my_source[:, None] * strip_rows + jnp.arange(strip_rows, dtype=jnp.int32)[None, :]
    ).reshape(slot_rows)
    even = (row_number[:, None] + jnp.arange(P_SIZE, dtype=jnp.int32)[None, :]) % 2 == 0
    out_real = jnp.where(even[None, :, :], plus_real, minus_real)
    out_imag = jnp.where(even[None, :, :], plus_imag, minus_imag)
    return jnp.stack([out_real, out_imag], axis=1)


def solution(mesh):
    placed = (P(None, "row", "col"), P(), P())
    return jax.shard_map(
        body,
        mesh=mesh,
        in_specs=placed,
        out_specs=P(None, None, ("row", "col"), None),
        check_vma=False,
    )
```

```python
import math

import jax
import jax.numpy as jnp
from jax import lax
from jax.sharding import PartitionSpec as P

H = 8192
S = 2048
P_SIZE = 4096
MOST = 3


two_pi = 2.0 * math.pi
radix = 128
headroom = 1.25
softness = 0.01
epsilon = 1e-06


def contract(form, left, right):
    return jnp.einsum(
        form, left, right, precision=lax.Precision.HIGH, preferred_element_type=jnp.float32
    )


def make_tables(frequency, in_len, length, offset, sign):
    accum = length // radix
    blocks = in_len // radix
    first = frequency[:, :accum] % accum
    inner_index = first[:, :, None] * jnp.arange(blocks, dtype=jnp.int32)[None, None, :] % accum
    inner_angle = sign * two_pi / accum * inner_index.astype(jnp.float32)
    column = (jnp.arange(radix, dtype=jnp.int32) + offset) % length
    outer_index = frequency[:, :, None] * column[None, None, :] % length
    outer_angle = sign * two_pi / length * outer_index.astype(jnp.float32)
    shape_four = (frequency.shape[0], frequency.shape[1] // accum, accum, radix)
    return lax.optimization_barrier(
        (
            jnp.cos(inner_angle),
            jnp.sin(inner_angle),
            jnp.cos(outer_angle).reshape(shape_four),
            jnp.sin(outer_angle).reshape(shape_four),
        )
    )


def transform(real_part, imag_part, tables, strip_major=False):
    inner_cos, inner_sin, outer_cos, outer_sin = tables
    batch, rows, width = real_part.shape
    blocks = width // radix
    real_four = real_part.reshape(batch, rows, blocks, radix)
    mid_real = contract("kpa,krab->krpb", inner_cos, real_four)
    mid_imag = contract("kpa,krab->krpb", inner_sin, real_four)
    if imag_part is not None:
        imag_four = imag_part.reshape(batch, rows, blocks, radix)
        mid_real = mid_real - contract("kpa,krab->krpb", inner_sin, imag_four)
        mid_imag = mid_imag + contract("kpa,krab->krpb", inner_cos, imag_four)
    form = "kqpb,krpb->qkrp" if strip_major else "kqpb,krpb->krqp"
    out_real = contract(form, outer_cos, mid_real) - contract(form, outer_sin, mid_imag)
    out_imag = contract(form, outer_cos, mid_imag) + contract(form, outer_sin, mid_real)
    if strip_major:
        return (out_real, out_imag)
    count = outer_cos.shape[1] * outer_cos.shape[2]
    return (out_real.reshape(batch, rows, count), out_imag.reshape(batch, rows, count))


def encode(field_real, field_imag, peak):
    scale = headroom * peak + epsilon
    unit_real = field_real / scale
    unit_imag = field_imag / scale
    square = unit_real * unit_real + unit_imag * unit_imag
    height = jnp.sqrt(1.0 - square)
    spread = jnp.sqrt(square + softness)
    phase_real = unit_real / spread
    phase_imag = unit_imag / spread
    plus_real = unit_real - phase_imag * height
    plus_imag = unit_imag + phase_real * height
    minus_real = unit_real + phase_imag * height
    minus_imag = unit_imag - phase_real * height
    return (plus_real, plus_imag, minus_real, minus_imag)


def body(holograms, sideband_centre, strip_owner):
    holo_count = holograms.shape[0]
    row_devices = lax.axis_size("row")
    col_devices = lax.axis_size("col")
    devices = row_devices * col_devices
    half = S // 2
    offsets = jnp.arange(S, dtype=jnp.int32) - half
    along_u = (sideband_centre[:, 0:1] + offsets[None, :]) % H
    along_v = (sideband_centre[:, 1:2] + offsets[None, :]) % H
    table_v = make_tables(along_v, H, H, 0, -1.0)
    table_u = make_tables(along_u, H, H, 0, -1.0)
    pixels = jnp.broadcast_to(jnp.arange(P_SIZE, dtype=jnp.int32)[None, :], (holo_count, P_SIZE))
    table_p = make_tables(pixels, S, P_SIZE, P_SIZE - half, 1.0)
    local_rows = holograms.shape[1]
    local_cols = holograms.shape[2]
    blocks = holograms.reshape(holo_count, col_devices, local_rows // col_devices, local_cols)
    piece = lax.all_to_all(blocks, "col", split_axis=1, concat_axis=3, tiled=True)
    lead, single, count, width = piece.shape
    out_real, out_imag = transform(piece.reshape(lead, count, width), None, table_v)
    spec_real = out_real.reshape(lead, single, count, S)
    spec_imag = out_imag.reshape(lead, single, count, S)
    pencil = spec_real.shape[2]
    share = S // devices
    col_real = jnp.swapaxes(spec_real.reshape(holo_count, pencil, S), 1, 2)
    col_imag = jnp.swapaxes(spec_imag.reshape(holo_count, pencil, S), 1, 2)
    piece_real = lax.all_to_all(
        col_real.reshape(holo_count, devices, share, pencil),
        ("row", "col"),
        split_axis=1,
        concat_axis=3,
        tiled=True,
    )
    piece_imag = lax.all_to_all(
        col_imag.reshape(holo_count, devices, share, pencil),
        ("row", "col"),
        split_axis=1,
        concat_axis=3,
        tiled=True,
    )
    lead, single, count, width = piece_real.shape
    out_real, out_imag = transform(
        piece_real.reshape(lead, count, width), piece_imag.reshape(lead, count, width), table_u
    )
    side_real = out_real.reshape(lead, single, count, S)
    side_imag = out_imag.reshape(lead, single, count, S)
    strips = strip_owner.shape[0]
    strip_rows = P_SIZE // strips
    slot_rows = MOST * strip_rows
    strip_ids = jnp.arange(strips, dtype=jnp.int32)
    same = strip_owner[:, None] == strip_owner[None, :]
    before = strip_ids[None, :] < strip_ids[:, None]
    rank = jnp.sum((same & before).astype(jnp.int32), axis=1)
    slot_of = strip_owner * MOST + rank
    slot_ids = jnp.arange(strips * MOST, dtype=jnp.int32)
    match = slot_of[None, :] == slot_ids[:, None]
    source = jnp.sum(jnp.where(match, strip_ids[None, :], 0), axis=1)
    filled = jnp.any(match, axis=1).astype(jnp.float32)
    by_strip = table_p[2].shape[2] == strip_rows and table_p[2].shape[1] == strips
    lift_real, lift_imag = transform(
        side_real.reshape(holo_count, share, S),
        side_imag.reshape(holo_count, share, S),
        table_p,
        strip_major=by_strip,
    )

    if by_strip:

        def pack(part):
            picked = jnp.take(part, source, axis=0) * filled[:, None, None, None]
            return picked.reshape(devices, MOST, holo_count, share, strip_rows)

        def unpack(piece):
            rows = jnp.transpose(piece, (2, 1, 4, 0, 3))
            return rows.reshape(holo_count, slot_rows, devices * share)

        piece_real = lax.all_to_all(pack(lift_real), ("row", "col"), 0, 0, tiled=True)
        piece_imag = lax.all_to_all(pack(lift_imag), ("row", "col"), 0, 0, tiled=True)
        rows_real = unpack(piece_real)
        rows_imag = unpack(piece_imag)
    else:

        def pack(part):
            grouped = part.reshape(holo_count, share, strips, strip_rows)
            picked = jnp.take(grouped, source, axis=2) * filled[None, None, :, None]
            return jnp.transpose(picked.reshape(holo_count, share, strips, slot_rows), (2, 0, 1, 3))

        def unpack(piece):
            single, lead, width, count = piece.shape
            return jnp.swapaxes(piece.reshape(lead, width, count), 1, 2)

        piece_real = lax.all_to_all(pack(lift_real), ("row", "col"), 0, 2, tiled=True)
        piece_imag = lax.all_to_all(pack(lift_imag), ("row", "col"), 0, 2, tiled=True)
        rows_real = unpack(piece_real)
        rows_imag = unpack(piece_imag)
    out_real, out_imag = transform(rows_real, rows_imag, table_p)
    field_real = out_real.reshape(holo_count, slot_rows, P_SIZE)
    field_imag = out_imag.reshape(holo_count, slot_rows, P_SIZE)
    magnitude = jnp.sqrt(field_real * field_real + field_imag * field_imag)
    local_peak = jnp.max(magnitude, axis=(1, 2))
    every = jnp.broadcast_to(local_peak[None, :], (devices, holo_count))
    peak = jnp.max(lax.all_to_all(every, ("row", "col"), 0, 0, tiled=True), axis=0)
    plus_real, plus_imag, minus_real, minus_imag = encode(
        field_real, field_imag, peak[:, None, None]
    )
    device_index = lax.axis_index("row") * col_devices + lax.axis_index("col")
    my_source = lax.dynamic_slice_in_dim(source, device_index * MOST, MOST)
    row_number = (
        my_source[:, None] * strip_rows + jnp.arange(strip_rows, dtype=jnp.int32)[None, :]
    ).reshape(slot_rows)
    even = (row_number[:, None] + jnp.arange(P_SIZE, dtype=jnp.int32)[None, :]) % 2 == 0
    out_real = jnp.where(even[None, :, :], plus_real, minus_real)
    out_imag = jnp.where(even[None, :, :], plus_imag, minus_imag)
    return jnp.stack([out_real, out_imag], axis=1)


def solution(mesh):
    placed = (P(None, "row", "col"), P(), P())
    return jax.shard_map(
        body,
        mesh=mesh,
        in_specs=placed,
        out_specs=P(None, None, ("row", "col"), None),
        check_vma=False,
    )
```

```python
import math

import jax
import jax.numpy as jnp
from jax import lax
from jax.sharding import PartitionSpec as P

H = 8192
S = 2048
P_SIZE = 4096
MOST = 3


two_pi = 2.0 * math.pi
radix = 128
headroom = 1.25
softness = 0.01
epsilon = 1e-06


def contract(form, left, right):
    return jnp.einsum(
        form, left, right, precision=lax.Precision.HIGH, preferred_element_type=jnp.float32
    )


def make_tables(frequency, in_len, length, offset, sign):
    accum = length // radix
    blocks = in_len // radix
    first = frequency[:, :accum] % accum
    inner_index = first[:, :, None] * jnp.arange(blocks, dtype=jnp.int32)[None, None, :] % accum
    inner_angle = sign * two_pi / accum * inner_index.astype(jnp.float32)
    column = (jnp.arange(radix, dtype=jnp.int32) + offset) % length
    outer_index = frequency[:, :, None] * column[None, None, :] % length
    outer_angle = sign * two_pi / length * outer_index.astype(jnp.float32)
    shape_four = (frequency.shape[0], frequency.shape[1] // accum, accum, radix)
    return lax.optimization_barrier(
        (
            jnp.cos(inner_angle),
            jnp.sin(inner_angle),
            jnp.cos(outer_angle).reshape(shape_four),
            jnp.sin(outer_angle).reshape(shape_four),
        )
    )


def transform(real_part, imag_part, tables):
    inner_cos, inner_sin, outer_cos, outer_sin = tables
    batch, rows, width = real_part.shape
    blocks = width // radix
    real_four = real_part.reshape(batch, rows, blocks, radix)
    mid_real = contract("kpa,krab->krpb", inner_cos, real_four)
    mid_imag = contract("kpa,krab->krpb", inner_sin, real_four)
    if imag_part is not None:
        imag_four = imag_part.reshape(batch, rows, blocks, radix)
        mid_real = mid_real - contract("kpa,krab->krpb", inner_sin, imag_four)
        mid_imag = mid_imag + contract("kpa,krab->krpb", inner_cos, imag_four)
    return finish(mid_real, mid_imag, tables)


def finish(mid_real, mid_imag, tables):
    inner_cos, inner_sin, outer_cos, outer_sin = tables
    batch, rows = mid_real.shape[:2]
    out_real = contract("kqpb,krpb->krqp", outer_cos, mid_real) - contract(
        "kqpb,krpb->krqp", outer_sin, mid_imag
    )
    out_imag = contract("kqpb,krpb->krqp", outer_cos, mid_imag) + contract(
        "kqpb,krpb->krqp", outer_sin, mid_real
    )
    count = outer_cos.shape[1] * outer_cos.shape[2]
    return (out_real.reshape(batch, rows, count), out_imag.reshape(batch, rows, count))


def encode(field_real, field_imag, peak):
    scale = headroom * peak + epsilon
    unit_real = field_real / scale
    unit_imag = field_imag / scale
    square = unit_real * unit_real + unit_imag * unit_imag
    height = jnp.sqrt(1.0 - square)
    spread = jnp.sqrt(square + softness)
    phase_real = unit_real / spread
    phase_imag = unit_imag / spread
    plus_real = unit_real - phase_imag * height
    plus_imag = unit_imag + phase_real * height
    minus_real = unit_real + phase_imag * height
    minus_imag = unit_imag - phase_real * height
    return (plus_real, plus_imag, minus_real, minus_imag)


def body(holograms, sideband_centre, strip_owner):
    holo_count = holograms.shape[0]
    row_devices = lax.axis_size("row")
    col_devices = lax.axis_size("col")
    devices = row_devices * col_devices
    half = S // 2
    offsets = jnp.arange(S, dtype=jnp.int32) - half
    along_u = (sideband_centre[:, 0:1] + offsets[None, :]) % H
    along_v = (sideband_centre[:, 1:2] + offsets[None, :]) % H
    table_v = make_tables(along_v, H, H, 0, -1.0)
    table_u = make_tables(along_u, H, H, 0, -1.0)
    pixels = jnp.broadcast_to(jnp.arange(P_SIZE, dtype=jnp.int32)[None, :], (holo_count, P_SIZE))
    table_p = make_tables(pixels, S, P_SIZE, P_SIZE - half, 1.0)
    local_rows = holograms.shape[1]
    local_cols = holograms.shape[2]
    blocks = holograms.reshape(holo_count, col_devices, local_rows // col_devices, local_cols)
    piece = lax.all_to_all(blocks, "col", split_axis=1, concat_axis=1, tiled=True)
    lead, senders, count, width = piece.shape
    single = 1
    sender_blocks = width // radix
    piece_five = piece.reshape(lead, senders, count, sender_blocks, radix)
    inner_cos, inner_sin = table_v[0], table_v[1]
    per_sender = inner_cos.shape[:2] + (senders, sender_blocks)
    mid_real = contract("kpjc,kjrcb->krpb", inner_cos.reshape(per_sender), piece_five)
    mid_imag = contract("kpjc,kjrcb->krpb", inner_sin.reshape(per_sender), piece_five)
    out_real, out_imag = finish(mid_real, mid_imag, table_v)
    spec_real = out_real.reshape(lead, single, count, S)
    spec_imag = out_imag.reshape(lead, single, count, S)
    pencil = spec_real.shape[2]
    share = S // devices
    col_real = jnp.swapaxes(spec_real.reshape(holo_count, pencil, S), 1, 2)
    col_imag = jnp.swapaxes(spec_imag.reshape(holo_count, pencil, S), 1, 2)
    piece_real = lax.all_to_all(
        col_real.reshape(holo_count, devices, share, pencil),
        ("row", "col"),
        split_axis=1,
        concat_axis=3,
        tiled=True,
    )
    piece_imag = lax.all_to_all(
        col_imag.reshape(holo_count, devices, share, pencil),
        ("row", "col"),
        split_axis=1,
        concat_axis=3,
        tiled=True,
    )
    lead, single, count, width = piece_real.shape
    out_real, out_imag = transform(
        piece_real.reshape(lead, count, width), piece_imag.reshape(lead, count, width), table_u
    )
    side_real = out_real.reshape(lead, single, count, S)
    side_imag = out_imag.reshape(lead, single, count, S)
    lift_real, lift_imag = transform(
        side_real.reshape(holo_count, share, S), side_imag.reshape(holo_count, share, S), table_p
    )
    strips = strip_owner.shape[0]
    strip_rows = P_SIZE // strips
    slot_rows = MOST * strip_rows
    strip_ids = jnp.arange(strips, dtype=jnp.int32)
    same = strip_owner[:, None] == strip_owner[None, :]
    before = strip_ids[None, :] < strip_ids[:, None]
    rank = jnp.sum((same & before).astype(jnp.int32), axis=1)
    slot_of = strip_owner * MOST + rank
    slot_ids = jnp.arange(strips * MOST, dtype=jnp.int32)
    match = slot_of[None, :] == slot_ids[:, None]
    source = jnp.sum(jnp.where(match, strip_ids[None, :], 0), axis=1)
    filled = jnp.any(match, axis=1).astype(jnp.float32)

    def pack(part):
        grouped = part.reshape(holo_count, share, strips, strip_rows)
        picked = jnp.take(grouped, source, axis=2) * filled[None, None, :, None]
        return jnp.transpose(picked.reshape(holo_count, share, strips, slot_rows), (2, 0, 1, 3))

    send_real = pack(lift_real)
    send_imag = pack(lift_imag)
    piece_real = lax.all_to_all(send_real, ("row", "col"), split_axis=0, concat_axis=2, tiled=True)
    piece_imag = lax.all_to_all(send_imag, ("row", "col"), split_axis=0, concat_axis=2, tiled=True)
    single, lead, width, count = piece_real.shape
    rows_real = jnp.swapaxes(piece_real.reshape(lead, width, count), 1, 2)
    rows_imag = jnp.swapaxes(piece_imag.reshape(lead, width, count), 1, 2)
    out_real, out_imag = transform(rows_real, rows_imag, table_p)
    field_real = out_real.reshape(single, lead, count, P_SIZE)
    field_imag = out_imag.reshape(single, lead, count, P_SIZE)
    field_real = field_real.reshape(holo_count, slot_rows, P_SIZE)
    field_imag = field_imag.reshape(holo_count, slot_rows, P_SIZE)
    magnitude = jnp.sqrt(field_real * field_real + field_imag * field_imag)
    local_peak = jnp.max(magnitude, axis=(1, 2))
    every = jnp.broadcast_to(local_peak[None, :], (devices, holo_count))
    peak = jnp.max(lax.all_to_all(every, ("row", "col"), 0, 0, tiled=True), axis=0)
    plus_real, plus_imag, minus_real, minus_imag = encode(
        field_real, field_imag, peak[:, None, None]
    )
    device_index = lax.axis_index("row") * col_devices + lax.axis_index("col")
    my_source = lax.dynamic_slice_in_dim(source, device_index * MOST, MOST)
    row_number = (
        my_source[:, None] * strip_rows + jnp.arange(strip_rows, dtype=jnp.int32)[None, :]
    ).reshape(slot_rows)
    even = (row_number[:, None] + jnp.arange(P_SIZE, dtype=jnp.int32)[None, :]) % 2 == 0
    out_real = jnp.where(even[None, :, :], plus_real, minus_real)
    out_imag = jnp.where(even[None, :, :], plus_imag, minus_imag)
    return jnp.stack([out_real, out_imag], axis=1)


def solution(mesh):
    placed = (P(None, "row", "col"), P(), P())
    return jax.shard_map(
        body,
        mesh=mesh,
        in_specs=placed,
        out_specs=P(None, None, ("row", "col"), None),
        check_vma=False,
    )
```

```python
import math

import jax
import jax.numpy as jnp
from jax import lax
from jax.sharding import PartitionSpec as P

H = 8192
S = 2048
P_SIZE = 4096
MOST = 3


two_pi = 2.0 * math.pi
radix = 128
headroom = 1.25
softness = 0.01
epsilon = 1e-06


def contract(form, left, right):
    return jnp.einsum(
        form, left, right, precision=lax.Precision.HIGH, preferred_element_type=jnp.float32
    )


def make_tables(frequency, in_len, length, offset, sign):
    accum = length // radix
    blocks = in_len // radix
    first = frequency[:, :accum] % accum
    inner_index = first[:, :, None] * jnp.arange(blocks, dtype=jnp.int32)[None, None, :] % accum
    inner_angle = sign * two_pi / accum * inner_index.astype(jnp.float32)
    column = (jnp.arange(radix, dtype=jnp.int32) + offset) % length
    outer_index = frequency[:, :, None] * column[None, None, :] % length
    outer_angle = sign * two_pi / length * outer_index.astype(jnp.float32)
    shape_four = (frequency.shape[0], frequency.shape[1] // accum, accum, radix)
    return lax.optimization_barrier(
        (
            jnp.cos(inner_angle),
            jnp.sin(inner_angle),
            jnp.cos(outer_angle).reshape(shape_four),
            jnp.sin(outer_angle).reshape(shape_four),
        )
    )


def transform(real_part, imag_part, tables):
    inner_cos, inner_sin, outer_cos, outer_sin = tables
    batch, rows, width = real_part.shape
    blocks = width // radix
    real_four = real_part.reshape(batch, rows, blocks, radix)
    mid_real = contract("kpa,krab->krpb", inner_cos, real_four)
    mid_imag = contract("kpa,krab->krpb", inner_sin, real_four)
    if imag_part is not None:
        imag_four = imag_part.reshape(batch, rows, blocks, radix)
        mid_real = mid_real - contract("kpa,krab->krpb", inner_sin, imag_four)
        mid_imag = mid_imag + contract("kpa,krab->krpb", inner_cos, imag_four)
    return finish(mid_real, mid_imag, tables)


def finish(mid_real, mid_imag, tables):
    inner_cos, inner_sin, outer_cos, outer_sin = tables
    batch, rows = mid_real.shape[:2]
    out_real = contract("kqpb,krpb->krqp", outer_cos, mid_real) - contract(
        "kqpb,krpb->krqp", outer_sin, mid_imag
    )
    out_imag = contract("kqpb,krpb->krqp", outer_cos, mid_imag) + contract(
        "kqpb,krpb->krqp", outer_sin, mid_real
    )
    count = outer_cos.shape[1] * outer_cos.shape[2]
    return (out_real.reshape(batch, rows, count), out_imag.reshape(batch, rows, count))


def encode(field_real, field_imag, peak):
    scale = headroom * peak + epsilon
    unit_real = field_real / scale
    unit_imag = field_imag / scale
    square = unit_real * unit_real + unit_imag * unit_imag
    height = jnp.sqrt(1.0 - square)
    spread = jnp.sqrt(square + softness)
    phase_real = unit_real / spread
    phase_imag = unit_imag / spread
    plus_real = unit_real - phase_imag * height
    plus_imag = unit_imag + phase_real * height
    minus_real = unit_real + phase_imag * height
    minus_imag = unit_imag - phase_real * height
    return (plus_real, plus_imag, minus_real, minus_imag)


def body(holograms, sideband_centre, strip_owner):
    holo_count = holograms.shape[0]
    row_devices = lax.axis_size("row")
    col_devices = lax.axis_size("col")
    devices = row_devices * col_devices
    half = S // 2
    offsets = jnp.arange(S, dtype=jnp.int32) - half
    along_u = (sideband_centre[:, 0:1] + offsets[None, :]) % H
    along_v = (sideband_centre[:, 1:2] + offsets[None, :]) % H
    table_v = make_tables(along_v, H, H, 0, -1.0)
    table_u = make_tables(along_u, H, H, 0, -1.0)
    pixels = jnp.broadcast_to(jnp.arange(P_SIZE, dtype=jnp.int32)[None, :], (holo_count, P_SIZE))
    table_p = make_tables(pixels, S, P_SIZE, P_SIZE - half, 1.0)
    local_rows = holograms.shape[1]
    local_cols = holograms.shape[2]
    blocks = holograms.reshape(holo_count, col_devices, local_rows // col_devices, local_cols)
    piece = lax.all_to_all(blocks, "col", split_axis=1, concat_axis=1, tiled=True)
    lead, senders, count, width = piece.shape
    single = 1
    sender_blocks = width // radix
    piece_five = piece.reshape(lead, senders, count, sender_blocks, radix)
    inner_cos, inner_sin = table_v[0], table_v[1]
    per_sender = inner_cos.shape[:2] + (senders, sender_blocks)
    mid_real = contract("kpjc,kjrcb->krpb", inner_cos.reshape(per_sender), piece_five)
    mid_imag = contract("kpjc,kjrcb->krpb", inner_sin.reshape(per_sender), piece_five)
    share = S // devices
    outer_cos, outer_sin = table_v[2], table_v[3]
    form = "kqpb,krpb->qpkr"
    spec_real = contract(form, outer_cos, mid_real) - contract(form, outer_sin, mid_imag)
    spec_imag = contract(form, outer_cos, mid_imag) + contract(form, outer_sin, mid_real)
    send_shape = (devices, share, holo_count, count)
    piece_real = lax.all_to_all(spec_real.reshape(send_shape), ("row", "col"), 0, 0, tiled=True)
    piece_imag = lax.all_to_all(spec_imag.reshape(send_shape), ("row", "col"), 0, 0, tiled=True)
    pair = radix // count
    col_blocks = devices // pair
    recv_shape = (col_blocks, pair, share, holo_count, count)
    recv_real = piece_real.reshape(recv_shape)
    recv_imag = piece_imag.reshape(recv_shape)
    inner_cos, inner_sin = table_u[0], table_u[1]
    step = "kpa,alskr->ksplr"
    mid_real = contract(step, inner_cos, recv_real) - contract(step, inner_sin, recv_imag)
    mid_imag = contract(step, inner_sin, recv_real) + contract(step, inner_cos, recv_imag)
    mid_shape = (holo_count, share, inner_cos.shape[1], radix)
    side_real, side_imag = finish(mid_real.reshape(mid_shape), mid_imag.reshape(mid_shape), table_u)
    lift_real, lift_imag = transform(
        side_real.reshape(holo_count, share, S), side_imag.reshape(holo_count, share, S), table_p
    )
    strips = strip_owner.shape[0]
    strip_rows = P_SIZE // strips
    slot_rows = MOST * strip_rows
    strip_ids = jnp.arange(strips, dtype=jnp.int32)
    same = strip_owner[:, None] == strip_owner[None, :]
    before = strip_ids[None, :] < strip_ids[:, None]
    rank = jnp.sum((same & before).astype(jnp.int32), axis=1)
    slot_of = strip_owner * MOST + rank
    slot_ids = jnp.arange(strips * MOST, dtype=jnp.int32)
    match = slot_of[None, :] == slot_ids[:, None]
    source = jnp.sum(jnp.where(match, strip_ids[None, :], 0), axis=1)
    filled = jnp.any(match, axis=1).astype(jnp.float32)

    def pack(part):
        grouped = part.reshape(holo_count, share, strips, strip_rows)
        picked = jnp.take(grouped, source, axis=2) * filled[None, None, :, None]
        return jnp.transpose(picked.reshape(holo_count, share, strips, slot_rows), (2, 0, 1, 3))

    send_real = pack(lift_real)
    send_imag = pack(lift_imag)
    piece_real = lax.all_to_all(send_real, ("row", "col"), split_axis=0, concat_axis=2, tiled=True)
    piece_imag = lax.all_to_all(send_imag, ("row", "col"), split_axis=0, concat_axis=2, tiled=True)
    single, lead, width, count = piece_real.shape
    rows_real = jnp.swapaxes(piece_real.reshape(lead, width, count), 1, 2)
    rows_imag = jnp.swapaxes(piece_imag.reshape(lead, width, count), 1, 2)
    out_real, out_imag = transform(rows_real, rows_imag, table_p)
    field_real = out_real.reshape(single, lead, count, P_SIZE)
    field_imag = out_imag.reshape(single, lead, count, P_SIZE)
    field_real = field_real.reshape(holo_count, slot_rows, P_SIZE)
    field_imag = field_imag.reshape(holo_count, slot_rows, P_SIZE)
    magnitude = jnp.sqrt(field_real * field_real + field_imag * field_imag)
    local_peak = jnp.max(magnitude, axis=(1, 2))
    every = jnp.broadcast_to(local_peak[None, :], (devices, holo_count))
    peak = jnp.max(lax.all_to_all(every, ("row", "col"), 0, 0, tiled=True), axis=0)
    plus_real, plus_imag, minus_real, minus_imag = encode(
        field_real, field_imag, peak[:, None, None]
    )
    device_index = lax.axis_index("row") * col_devices + lax.axis_index("col")
    my_source = lax.dynamic_slice_in_dim(source, device_index * MOST, MOST)
    row_number = (
        my_source[:, None] * strip_rows + jnp.arange(strip_rows, dtype=jnp.int32)[None, :]
    ).reshape(slot_rows)
    even = (row_number[:, None] + jnp.arange(P_SIZE, dtype=jnp.int32)[None, :]) % 2 == 0
    out_real = jnp.where(even[None, :, :], plus_real, minus_real)
    out_imag = jnp.where(even[None, :, :], plus_imag, minus_imag)
    return jnp.stack([out_real, out_imag], axis=1)


def solution(mesh):
    placed = (P(None, "row", "col"), P(), P())
    return jax.shard_map(
        body,
        mesh=mesh,
        in_specs=placed,
        out_specs=P(None, None, ("row", "col"), None),
        check_vma=False,
    )
```

```python
import math

import jax
import jax.numpy as jnp
from jax import lax
from jax.sharding import PartitionSpec as P

H = 8192
S = 2048
P_SIZE = 4096
MOST = 3


two_pi = 2.0 * math.pi
radix = 128
headroom = 1.25
softness = 0.01
epsilon = 1e-06


def contract(form, left, right):
    return jnp.einsum(
        form, left, right, precision=lax.Precision.HIGH, preferred_element_type=jnp.float32
    )


def make_tables(frequency, in_len, length, offset, sign):
    accum = length // radix
    blocks = in_len // radix
    first = frequency[:, :accum] % accum
    inner_index = first[:, :, None] * jnp.arange(blocks, dtype=jnp.int32)[None, None, :] % accum
    inner_angle = sign * two_pi / accum * inner_index.astype(jnp.float32)
    column = (jnp.arange(radix, dtype=jnp.int32) + offset) % length
    outer_index = frequency[:, :, None] * column[None, None, :] % length
    outer_angle = sign * two_pi / length * outer_index.astype(jnp.float32)
    shape_four = (frequency.shape[0], frequency.shape[1] // accum, accum, radix)
    return lax.optimization_barrier(
        (
            jnp.cos(inner_angle),
            jnp.sin(inner_angle),
            jnp.cos(outer_angle).reshape(shape_four),
            jnp.sin(outer_angle).reshape(shape_four),
        )
    )


def transform(real_part, imag_part, tables):
    inner_cos, inner_sin, outer_cos, outer_sin = tables
    batch, rows, width = real_part.shape
    blocks = width // radix
    real_four = real_part.reshape(batch, rows, blocks, radix)
    mid_real = contract("kpa,krab->krpb", inner_cos, real_four)
    mid_imag = contract("kpa,krab->krpb", inner_sin, real_four)
    if imag_part is not None:
        imag_four = imag_part.reshape(batch, rows, blocks, radix)
        mid_real = mid_real - contract("kpa,krab->krpb", inner_sin, imag_four)
        mid_imag = mid_imag + contract("kpa,krab->krpb", inner_cos, imag_four)
    return finish(mid_real, mid_imag, tables)


def finish(mid_real, mid_imag, tables):
    inner_cos, inner_sin, outer_cos, outer_sin = tables
    batch, rows = mid_real.shape[:2]
    out_real = contract("kqpb,krpb->krqp", outer_cos, mid_real) - contract(
        "kqpb,krpb->krqp", outer_sin, mid_imag
    )
    out_imag = contract("kqpb,krpb->krqp", outer_cos, mid_imag) + contract(
        "kqpb,krpb->krqp", outer_sin, mid_real
    )
    count = outer_cos.shape[1] * outer_cos.shape[2]
    return (out_real.reshape(batch, rows, count), out_imag.reshape(batch, rows, count))


def encode(field_real, field_imag, peak):
    scale = headroom * peak + epsilon
    unit_real = field_real / scale
    unit_imag = field_imag / scale
    square = unit_real * unit_real + unit_imag * unit_imag
    height = jnp.sqrt(1.0 - square)
    spread = jnp.sqrt(square + softness)
    phase_real = unit_real / spread
    phase_imag = unit_imag / spread
    plus_real = unit_real - phase_imag * height
    plus_imag = unit_imag + phase_real * height
    minus_real = unit_real + phase_imag * height
    minus_imag = unit_imag - phase_real * height
    return (plus_real, plus_imag, minus_real, minus_imag)


def body(holograms, sideband_centre, strip_owner):
    holo_count = holograms.shape[0]
    row_devices = lax.axis_size("row")
    col_devices = lax.axis_size("col")
    devices = row_devices * col_devices
    half = S // 2
    offsets = jnp.arange(S, dtype=jnp.int32) - half
    along_u = (sideband_centre[:, 0:1] + offsets[None, :]) % H
    along_v = (sideband_centre[:, 1:2] + offsets[None, :]) % H
    table_v = make_tables(along_v, H, H, 0, -1.0)
    table_u = make_tables(along_u, H, H, 0, -1.0)
    pixels = jnp.broadcast_to(jnp.arange(P_SIZE, dtype=jnp.int32)[None, :], (holo_count, P_SIZE))
    table_p = make_tables(pixels, S, P_SIZE, P_SIZE - half, 1.0)
    local_rows = holograms.shape[1]
    local_cols = holograms.shape[2]
    blocks = holograms.reshape(holo_count, col_devices, local_rows // col_devices, local_cols)
    piece = lax.all_to_all(blocks, "col", split_axis=1, concat_axis=1, tiled=True)
    lead, senders, count, width = piece.shape
    single = 1
    sender_blocks = width // radix
    piece_five = piece.reshape(lead, senders, count, sender_blocks, radix)
    inner_cos, inner_sin = table_v[0], table_v[1]
    per_sender = inner_cos.shape[:2] + (senders, sender_blocks)
    mid_real = contract("kpjc,kjrcb->krpb", inner_cos.reshape(per_sender), piece_five)
    mid_imag = contract("kpjc,kjrcb->krpb", inner_sin.reshape(per_sender), piece_five)
    share = S // devices
    outer_cos, outer_sin = table_v[2], table_v[3]
    form = "kqpb,krpb->qpkr"
    spec_real = contract(form, outer_cos, mid_real) - contract(form, outer_sin, mid_imag)
    spec_imag = contract(form, outer_cos, mid_imag) + contract(form, outer_sin, mid_real)
    send_shape = (devices, share, holo_count, count)
    piece_real = lax.all_to_all(spec_real.reshape(send_shape), ("row", "col"), 0, 0, tiled=True)
    piece_imag = lax.all_to_all(spec_imag.reshape(send_shape), ("row", "col"), 0, 0, tiled=True)
    pair = radix // count
    col_blocks = devices // pair
    recv_shape = (col_blocks, pair, share, holo_count, count)
    recv_real = piece_real.reshape(recv_shape)
    recv_imag = piece_imag.reshape(recv_shape)
    inner_cos, inner_sin = table_u[0], table_u[1]
    step = "kpa,alskr->ksplr"
    mid_real = contract(step, inner_cos, recv_real) - contract(step, inner_sin, recv_imag)
    mid_imag = contract(step, inner_sin, recv_real) + contract(step, inner_cos, recv_imag)
    mid_shape = (holo_count, share, inner_cos.shape[1], radix)
    side_real, side_imag = finish(mid_real.reshape(mid_shape), mid_imag.reshape(mid_shape), table_u)
    strips = strip_owner.shape[0]
    strip_rows = P_SIZE // strips
    slot_rows = MOST * strip_rows
    strip_ids = jnp.arange(strips, dtype=jnp.int32)
    same = strip_owner[:, None] == strip_owner[None, :]
    before = strip_ids[None, :] < strip_ids[:, None]
    rank = jnp.sum((same & before).astype(jnp.int32), axis=1)
    slot_of = strip_owner * MOST + rank
    slot_ids = jnp.arange(strips * MOST, dtype=jnp.int32)
    match = slot_of[None, :] == slot_ids[:, None]
    source = jnp.sum(jnp.where(match, strip_ids[None, :], 0), axis=1)
    filled = jnp.any(match, axis=1).astype(jnp.float32)

    inner_cos, inner_sin, outer_cos, outer_sin = table_p
    side_shape = (holo_count, share, S // radix, radix)
    side_real = side_real.reshape(side_shape)
    side_imag = side_imag.reshape(side_shape)
    step = "kpa,krab->krpb"
    mid_real = contract(step, inner_cos, side_real) - contract(step, inner_sin, side_imag)
    mid_imag = contract(step, inner_sin, side_real) + contract(step, inner_cos, side_imag)
    form = "kqpb,krpb->qpkr"
    lift_real = contract(form, outer_cos, mid_real) - contract(form, outer_sin, mid_imag)
    lift_imag = contract(form, outer_cos, mid_imag) + contract(form, outer_sin, mid_real)

    def pack(part):
        grouped = part.reshape(strips, strip_rows, holo_count, share)
        picked = jnp.take(grouped, source, axis=0) * filled[:, None, None, None]
        return picked.reshape(devices, MOST, strip_rows, holo_count, share)

    piece_real = lax.all_to_all(pack(lift_real), ("row", "col"), 0, 0, tiled=True)
    piece_imag = lax.all_to_all(pack(lift_imag), ("row", "col"), 0, 0, tiled=True)
    pair = radix // share
    recv_shape = (devices // pair, pair, MOST, strip_rows, holo_count, share)
    recv_real = piece_real.reshape(recv_shape)
    recv_imag = piece_imag.reshape(recv_shape)
    step = "kpa,aoltks->kltpos"
    mid_real = contract(step, inner_cos, recv_real) - contract(step, inner_sin, recv_imag)
    mid_imag = contract(step, inner_sin, recv_real) + contract(step, inner_cos, recv_imag)
    mid_shape = (holo_count, slot_rows, inner_cos.shape[1], radix)
    field_real, field_imag = finish(mid_real.reshape(mid_shape), mid_imag.reshape(mid_shape), table_p)
    magnitude = jnp.sqrt(field_real * field_real + field_imag * field_imag)
    local_peak = jnp.max(magnitude, axis=(1, 2))
    every = jnp.broadcast_to(local_peak[None, :], (devices, holo_count))
    peak = jnp.max(lax.all_to_all(every, ("row", "col"), 0, 0, tiled=True), axis=0)
    plus_real, plus_imag, minus_real, minus_imag = encode(
        field_real, field_imag, peak[:, None, None]
    )
    device_index = lax.axis_index("row") * col_devices + lax.axis_index("col")
    my_source = lax.dynamic_slice_in_dim(source, device_index * MOST, MOST)
    row_number = (
        my_source[:, None] * strip_rows + jnp.arange(strip_rows, dtype=jnp.int32)[None, :]
    ).reshape(slot_rows)
    even = (row_number[:, None] + jnp.arange(P_SIZE, dtype=jnp.int32)[None, :]) % 2 == 0
    out_real = jnp.where(even[None, :, :], plus_real, minus_real)
    out_imag = jnp.where(even[None, :, :], plus_imag, minus_imag)
    return jnp.stack([out_real, out_imag], axis=1)


def solution(mesh):
    placed = (P(None, "row", "col"), P(), P())
    return jax.shard_map(
        body,
        mesh=mesh,
        in_specs=placed,
        out_specs=P(None, None, ("row", "col"), None),
        check_vma=False,
    )
```

```python
import math

import jax
import jax.numpy as jnp
from jax import lax
from jax.sharding import PartitionSpec as P

H = 8192
S = 2048
P_SIZE = 4096
MOST = 3


two_pi = 2.0 * math.pi
radix = 128
headroom = 1.25
softness = 0.01
epsilon = 1e-06


def contract(form, left, right):
    return jnp.einsum(
        form, left, right, precision=lax.Precision.HIGH, preferred_element_type=jnp.float32
    )


def make_tables(frequency, in_len, length, offset, sign):
    accum = length // radix
    blocks = in_len // radix
    first = frequency[:, :accum] % accum
    inner_index = first[:, :, None] * jnp.arange(blocks, dtype=jnp.int32)[None, None, :] % accum
    inner_angle = sign * two_pi / accum * inner_index.astype(jnp.float32)
    column = (jnp.arange(radix, dtype=jnp.int32) + offset) % length
    outer_index = frequency[:, :, None] * column[None, None, :] % length
    outer_angle = sign * two_pi / length * outer_index.astype(jnp.float32)
    shape_four = (frequency.shape[0], frequency.shape[1] // accum, accum, radix)
    return lax.optimization_barrier(
        (
            jnp.cos(inner_angle),
            jnp.sin(inner_angle),
            jnp.cos(outer_angle).reshape(shape_four),
            jnp.sin(outer_angle).reshape(shape_four),
        )
    )


def transform(real_part, imag_part, tables):
    inner_cos, inner_sin, outer_cos, outer_sin = tables
    batch, rows, width = real_part.shape
    blocks = width // radix
    real_four = real_part.reshape(batch, rows, blocks, radix)
    mid_real = contract("kpa,krab->krpb", inner_cos, real_four)
    mid_imag = contract("kpa,krab->krpb", inner_sin, real_four)
    if imag_part is not None:
        imag_four = imag_part.reshape(batch, rows, blocks, radix)
        mid_real = mid_real - contract("kpa,krab->krpb", inner_sin, imag_four)
        mid_imag = mid_imag + contract("kpa,krab->krpb", inner_cos, imag_four)
    return finish(mid_real, mid_imag, tables)


def finish(mid_real, mid_imag, tables):
    inner_cos, inner_sin, outer_cos, outer_sin = tables
    batch, rows = mid_real.shape[:2]
    out_real = contract("kqpb,krpb->krqp", outer_cos, mid_real) - contract(
        "kqpb,krpb->krqp", outer_sin, mid_imag
    )
    out_imag = contract("kqpb,krpb->krqp", outer_cos, mid_imag) + contract(
        "kqpb,krpb->krqp", outer_sin, mid_real
    )
    count = outer_cos.shape[1] * outer_cos.shape[2]
    return (out_real.reshape(batch, rows, count), out_imag.reshape(batch, rows, count))


def encode(field_real, field_imag, peak):
    scale = headroom * peak + epsilon
    unit_real = field_real / scale
    unit_imag = field_imag / scale
    square = unit_real * unit_real + unit_imag * unit_imag
    height = jnp.sqrt(1.0 - square)
    spread = jnp.sqrt(square + softness)
    phase_real = unit_real / spread
    phase_imag = unit_imag / spread
    plus_real = unit_real - phase_imag * height
    plus_imag = unit_imag + phase_real * height
    minus_real = unit_real + phase_imag * height
    minus_imag = unit_imag - phase_real * height
    return (plus_real, plus_imag, minus_real, minus_imag)


def body(holograms, sideband_centre, strip_owner):
    holo_count = holograms.shape[0]
    row_devices = lax.axis_size("row")
    col_devices = lax.axis_size("col")
    devices = row_devices * col_devices
    half = S // 2
    offsets = jnp.arange(S, dtype=jnp.int32) - half
    along_u = (sideband_centre[:, 0:1] + offsets[None, :]) % H
    along_v = (sideband_centre[:, 1:2] + offsets[None, :]) % H
    table_v = make_tables(along_v, H, H, 0, -1.0)
    table_u = make_tables(along_u, H, H, 0, -1.0)
    pixels = jnp.broadcast_to(jnp.arange(P_SIZE, dtype=jnp.int32)[None, :], (holo_count, P_SIZE))
    table_p = make_tables(pixels, S, P_SIZE, P_SIZE - half, 1.0)
    local_rows = holograms.shape[1]
    local_cols = holograms.shape[2]
    blocks = holograms.reshape(holo_count, col_devices, local_rows // col_devices, local_cols)
    piece = lax.all_to_all(blocks, "col", split_axis=1, concat_axis=1, tiled=True)
    lead, senders, count, width = piece.shape
    single = 1
    sender_blocks = width // radix
    piece_five = piece.reshape(lead, senders, count, sender_blocks, radix)
    inner_cos, inner_sin = table_v[0], table_v[1]
    per_sender = inner_cos.shape[:2] + (senders, sender_blocks)
    mid_real = contract("kpjc,kjrcb->krpb", inner_cos.reshape(per_sender), piece_five)
    mid_imag = contract("kpjc,kjrcb->krpb", inner_sin.reshape(per_sender), piece_five)
    share = S // devices
    outer_cos, outer_sin = table_v[2], table_v[3]
    form = "kqpb,krpb->qpkr"
    spec_real = contract(form, outer_cos, mid_real) - contract(form, outer_sin, mid_imag)
    spec_imag = contract(form, outer_cos, mid_imag) + contract(form, outer_sin, mid_real)
    send_shape = (devices, share, holo_count, count)
    piece_real = lax.all_to_all(spec_real.reshape(send_shape), ("row", "col"), 0, 0, tiled=True)
    piece_imag = lax.all_to_all(spec_imag.reshape(send_shape), ("row", "col"), 0, 0, tiled=True)
    pair = radix // count
    col_blocks = devices // pair
    recv_shape = (col_blocks, pair, share, holo_count, count)
    recv_real = piece_real.reshape(recv_shape)
    recv_imag = piece_imag.reshape(recv_shape)
    inner_cos, inner_sin = table_u[0], table_u[1]
    step = "kpa,alskr->ksplr"
    mid_real = contract(step, inner_cos, recv_real) - contract(step, inner_sin, recv_imag)
    mid_imag = contract(step, inner_sin, recv_real) + contract(step, inner_cos, recv_imag)
    mid_shape = (holo_count, share, inner_cos.shape[1], radix)
    side_real, side_imag = finish(mid_real.reshape(mid_shape), mid_imag.reshape(mid_shape), table_u)
    strips = strip_owner.shape[0]
    strip_rows = P_SIZE // strips
    slot_rows = MOST * strip_rows
    strip_ids = jnp.arange(strips, dtype=jnp.int32)
    same = strip_owner[:, None] == strip_owner[None, :]
    before = strip_ids[None, :] < strip_ids[:, None]
    rank = jnp.sum((same & before).astype(jnp.int32), axis=1)
    slot_of = strip_owner * MOST + rank
    slot_ids = jnp.arange(strips * MOST, dtype=jnp.int32)
    match = slot_of[None, :] == slot_ids[:, None]
    source = jnp.sum(jnp.where(match, strip_ids[None, :], 0), axis=1)
    filled = jnp.any(match, axis=1).astype(jnp.float32)

    inner_cos, inner_sin, outer_cos, outer_sin = table_p
    side_shape = (holo_count, share, S // radix, radix)
    side_real = side_real.reshape(side_shape)
    side_imag = side_imag.reshape(side_shape)
    step = "kpa,krab->krpb"
    mid_real = contract(step, inner_cos, side_real) - contract(step, inner_sin, side_imag)
    mid_imag = contract(step, inner_sin, side_real) + contract(step, inner_cos, side_imag)
    form = "kqpb,krpb->qkrp"
    lift_real = contract(form, outer_cos, mid_real) - contract(form, outer_sin, mid_imag)
    lift_imag = contract(form, outer_cos, mid_imag) + contract(form, outer_sin, mid_real)

    def pack(part):
        grouped = part.reshape(strips, holo_count, share, strip_rows)
        picked = jnp.take(grouped, source, axis=0) * filled[:, None, None, None]
        picked = picked.reshape(devices, MOST, holo_count, share, strip_rows)
        return jnp.transpose(picked, (0, 2, 3, 1, 4)).reshape(devices, holo_count, share, slot_rows)

    send_real = pack(lift_real)
    send_imag = pack(lift_imag)
    piece_real = lax.all_to_all(send_real, ("row", "col"), split_axis=0, concat_axis=2, tiled=True)
    piece_imag = lax.all_to_all(send_imag, ("row", "col"), split_axis=0, concat_axis=2, tiled=True)
    single, lead, width, count = piece_real.shape
    rows_real = jnp.swapaxes(piece_real.reshape(lead, width, count), 1, 2)
    rows_imag = jnp.swapaxes(piece_imag.reshape(lead, width, count), 1, 2)
    out_real, out_imag = transform(rows_real, rows_imag, table_p)
    field_real = out_real.reshape(single, lead, count, P_SIZE)
    field_imag = out_imag.reshape(single, lead, count, P_SIZE)
    field_real = field_real.reshape(holo_count, slot_rows, P_SIZE)
    field_imag = field_imag.reshape(holo_count, slot_rows, P_SIZE)
    magnitude = jnp.sqrt(field_real * field_real + field_imag * field_imag)
    local_peak = jnp.max(magnitude, axis=(1, 2))
    every = jnp.broadcast_to(local_peak[None, :], (devices, holo_count))
    peak = jnp.max(lax.all_to_all(every, ("row", "col"), 0, 0, tiled=True), axis=0)
    plus_real, plus_imag, minus_real, minus_imag = encode(
        field_real, field_imag, peak[:, None, None]
    )
    device_index = lax.axis_index("row") * col_devices + lax.axis_index("col")
    my_source = lax.dynamic_slice_in_dim(source, device_index * MOST, MOST)
    row_number = (
        my_source[:, None] * strip_rows + jnp.arange(strip_rows, dtype=jnp.int32)[None, :]
    ).reshape(slot_rows)
    even = (row_number[:, None] + jnp.arange(P_SIZE, dtype=jnp.int32)[None, :]) % 2 == 0
    out_real = jnp.where(even[None, :, :], plus_real, minus_real)
    out_imag = jnp.where(even[None, :, :], plus_imag, minus_imag)
    return jnp.stack([out_real, out_imag], axis=1)


def solution(mesh):
    placed = (P(None, "row", "col"), P(), P())
    return jax.shard_map(
        body,
        mesh=mesh,
        in_specs=placed,
        out_specs=P(None, None, ("row", "col"), None),
        check_vma=False,
    )
```

```python
import math

import jax
import jax.numpy as jnp
from jax import lax
from jax.experimental import pallas as pl
from jax.experimental.pallas import tpu as pltpu
from jax.sharding import PartitionSpec as P

H = 8192
S = 2048
P_SIZE = 4096
MOST = 3


two_pi = 2.0 * math.pi
radix = 128
headroom = 1.25
softness = 0.01
epsilon = 1e-06


def contract(form, left, right):
    return jnp.einsum(
        form, left, right, precision=lax.Precision.HIGH, preferred_element_type=jnp.float32
    )


def make_tables(frequency, in_len, length, offset, sign):
    accum = length // radix
    blocks = in_len // radix
    first = frequency[:, :accum] % accum
    inner_index = first[:, :, None] * jnp.arange(blocks, dtype=jnp.int32)[None, None, :] % accum
    inner_angle = sign * two_pi / accum * inner_index.astype(jnp.float32)
    column = (jnp.arange(radix, dtype=jnp.int32) + offset) % length
    outer_index = frequency[:, :, None] * column[None, None, :] % length
    outer_angle = sign * two_pi / length * outer_index.astype(jnp.float32)
    shape_four = (frequency.shape[0], frequency.shape[1] // accum, accum, radix)
    return lax.optimization_barrier(
        (
            jnp.cos(inner_angle),
            jnp.sin(inner_angle),
            jnp.cos(outer_angle).reshape(shape_four),
            jnp.sin(outer_angle).reshape(shape_four),
        )
    )


def transform(real_part, imag_part, tables):
    inner_cos, inner_sin, outer_cos, outer_sin = tables
    batch, rows, width = real_part.shape
    blocks = width // radix
    real_four = real_part.reshape(batch, rows, blocks, radix)
    mid_real = contract("kpa,krab->krpb", inner_cos, real_four)
    mid_imag = contract("kpa,krab->krpb", inner_sin, real_four)
    if imag_part is not None:
        imag_four = imag_part.reshape(batch, rows, blocks, radix)
        mid_real = mid_real - contract("kpa,krab->krpb", inner_sin, imag_four)
        mid_imag = mid_imag + contract("kpa,krab->krpb", inner_cos, imag_four)
    return finish(mid_real, mid_imag, tables)


def finish(mid_real, mid_imag, tables):
    inner_cos, inner_sin, outer_cos, outer_sin = tables
    batch, rows = mid_real.shape[:2]
    out_real = contract("kqpb,krpb->krqp", outer_cos, mid_real) - contract(
        "kqpb,krpb->krqp", outer_sin, mid_imag
    )
    out_imag = contract("kqpb,krpb->krqp", outer_cos, mid_imag) + contract(
        "kqpb,krpb->krqp", outer_sin, mid_real
    )
    count = outer_cos.shape[1] * outer_cos.shape[2]
    return (out_real.reshape(batch, rows, count), out_imag.reshape(batch, rows, count))


def encode(field_real, field_imag, peak):
    scale = headroom * peak + epsilon
    unit_real = field_real / scale
    unit_imag = field_imag / scale
    square = unit_real * unit_real + unit_imag * unit_imag
    height = jnp.sqrt(1.0 - square)
    spread = jnp.sqrt(square + softness)
    phase_real = unit_real / spread
    phase_imag = unit_imag / spread
    plus_real = unit_real - phase_imag * height
    plus_imag = unit_imag + phase_real * height
    minus_real = unit_real + phase_imag * height
    minus_imag = unit_imag - phase_real * height
    return (plus_real, plus_imag, minus_real, minus_imag)


def body(holograms, sideband_centre, strip_owner):
    holo_count = holograms.shape[0]
    row_devices = lax.axis_size("row")
    col_devices = lax.axis_size("col")
    devices = row_devices * col_devices
    half = S // 2
    offsets = jnp.arange(S, dtype=jnp.int32) - half
    along_u = (sideband_centre[:, 0:1] + offsets[None, :]) % H
    along_v = (sideband_centre[:, 1:2] + offsets[None, :]) % H
    table_v = make_tables(along_v, H, H, 0, -1.0)
    table_u = make_tables(along_u, H, H, 0, -1.0)
    pixels = jnp.broadcast_to(jnp.arange(P_SIZE, dtype=jnp.int32)[None, :], (holo_count, P_SIZE))
    table_p = make_tables(pixels, S, P_SIZE, P_SIZE - half, 1.0)
    local_rows = holograms.shape[1]
    local_cols = holograms.shape[2]
    blocks = holograms.reshape(holo_count, col_devices, local_rows // col_devices, local_cols)
    piece = lax.all_to_all(blocks, "col", split_axis=1, concat_axis=1, tiled=True)
    lead, senders, count, width = piece.shape
    single = 1
    sender_blocks = width // radix
    piece_five = piece.reshape(lead, senders, count, sender_blocks, radix)
    inner_cos, inner_sin = table_v[0], table_v[1]
    per_sender = inner_cos.shape[:2] + (senders, sender_blocks)
    mid_real = contract("kpjc,kjrcb->krpb", inner_cos.reshape(per_sender), piece_five)
    mid_imag = contract("kpjc,kjrcb->krpb", inner_sin.reshape(per_sender), piece_five)
    share = S // devices
    outer_cos, outer_sin = table_v[2], table_v[3]
    form = "kqpb,krpb->qpkr"
    spec_real = contract(form, outer_cos, mid_real) - contract(form, outer_sin, mid_imag)
    spec_imag = contract(form, outer_cos, mid_imag) + contract(form, outer_sin, mid_real)
    send_shape = (devices, share, holo_count, count)
    piece_real = lax.all_to_all(spec_real.reshape(send_shape), ("row", "col"), 0, 0, tiled=True)
    piece_imag = lax.all_to_all(spec_imag.reshape(send_shape), ("row", "col"), 0, 0, tiled=True)
    pair = radix // count
    col_blocks = devices // pair
    recv_shape = (col_blocks, pair, share, holo_count, count)
    recv_real = piece_real.reshape(recv_shape)
    recv_imag = piece_imag.reshape(recv_shape)
    inner_cos, inner_sin = table_u[0], table_u[1]
    step = "kpa,alskr->ksplr"
    mid_real = contract(step, inner_cos, recv_real) - contract(step, inner_sin, recv_imag)
    mid_imag = contract(step, inner_sin, recv_real) + contract(step, inner_cos, recv_imag)
    mid_shape = (holo_count, share, inner_cos.shape[1], radix)
    side_real, side_imag = finish(mid_real.reshape(mid_shape), mid_imag.reshape(mid_shape), table_u)
    lift_real, lift_imag = transform(
        side_real.reshape(holo_count, share, S), side_imag.reshape(holo_count, share, S), table_p
    )
    strips = strip_owner.shape[0]
    strip_rows = P_SIZE // strips
    slot_rows = MOST * strip_rows
    strip_ids = jnp.arange(strips, dtype=jnp.int32)
    same = strip_owner[:, None] == strip_owner[None, :]
    before = strip_ids[None, :] < strip_ids[:, None]
    rank = jnp.sum((same & before).astype(jnp.int32), axis=1)
    slot_of = strip_owner * MOST + rank
    slot_ids = jnp.arange(strips * MOST, dtype=jnp.int32)
    match = slot_of[None, :] == slot_ids[:, None]
    source = jnp.sum(jnp.where(match, strip_ids[None, :], 0), axis=1)
    filled = jnp.any(match, axis=1).astype(jnp.float32)

    def pack(part):
        grouped = part.reshape(holo_count, share, strips, strip_rows)
        picked = jnp.take(grouped, source, axis=2) * filled[None, None, :, None]
        return jnp.transpose(picked.reshape(holo_count, share, strips, slot_rows), (2, 0, 1, 3))

    send_real = pack(lift_real)
    send_imag = pack(lift_imag)
    piece_real = lax.all_to_all(send_real, ("row", "col"), split_axis=0, concat_axis=2, tiled=True)
    piece_imag = lax.all_to_all(send_imag, ("row", "col"), split_axis=0, concat_axis=2, tiled=True)
    single, lead, width, count = piece_real.shape
    rows_real = jnp.swapaxes(piece_real.reshape(lead, width, count), 1, 2)
    rows_imag = jnp.swapaxes(piece_imag.reshape(lead, width, count), 1, 2)
    out_real, out_imag = transform(rows_real, rows_imag, table_p)
    field_real = out_real.reshape(single, lead, count, P_SIZE)
    field_imag = out_imag.reshape(single, lead, count, P_SIZE)
    field_real = field_real.reshape(holo_count, slot_rows, P_SIZE)
    field_imag = field_imag.reshape(holo_count, slot_rows, P_SIZE)
    magnitude = jnp.sqrt(field_real * field_real + field_imag * field_imag)
    local_peak = jnp.max(magnitude, axis=(1, 2))
    every = jnp.broadcast_to(local_peak[None, :], (devices, holo_count))
    peak = jnp.max(lax.all_to_all(every, ("row", "col"), 0, 0, tiled=True), axis=0)
    device_index = lax.axis_index("row") * col_devices + lax.axis_index("col")
    my_source = lax.dynamic_slice_in_dim(source, device_index * MOST, MOST)
    row_number = (
        my_source[:, None] * strip_rows + jnp.arange(strip_rows, dtype=jnp.int32)[None, :]
    ).reshape(slot_rows)
    parity = (row_number % 2)[:, None]
    return encode_slots(peak, parity, field_real, field_imag)


def encode_kernel(peak_ref, parity_ref, real_ref, imag_ref, out_ref):
    peak = peak_ref[pl.program_id(0)]
    plus_real, plus_imag, minus_real, minus_imag = encode(real_ref[0], imag_ref[0], peak)
    column = lax.broadcasted_iota(jnp.int32, plus_real.shape, 1)
    even = (parity_ref[...] + column) % 2 == 0
    out_ref[0, 0] = jnp.where(even, plus_real, minus_real)
    out_ref[0, 1] = jnp.where(even, plus_imag, minus_imag)


def encode_slots(peak, parity, field_real, field_imag):
    holo_count, rows, width = field_real.shape
    split = 2 if rows % 16 == 0 else 1
    block = rows // split
    field_spec = pl.BlockSpec((1, block, width), lambda k, j: (k, j, 0))
    return pl.pallas_call(
        encode_kernel,
        out_shape=jax.ShapeDtypeStruct((holo_count, 2, rows, width), jnp.float32),
        grid=(holo_count, split),
        in_specs=[
            pl.BlockSpec(memory_space=pltpu.SMEM),
            pl.BlockSpec((block, 1), lambda k, j: (j, 0)),
            field_spec,
            field_spec,
        ],
        out_specs=pl.BlockSpec((1, 2, block, width), lambda k, j: (k, 0, j, 0)),
    )(peak, parity, field_real, field_imag)


def solution(mesh):
    placed = (P(None, "row", "col"), P(), P())
    return jax.shard_map(
        body,
        mesh=mesh,
        in_specs=placed,
        out_specs=P(None, None, ("row", "col"), None),
        check_vma=False,
    )
```

```python
import math

import jax
import jax.numpy as jnp
from jax import lax
from jax.experimental import pallas as pl
from jax.experimental.pallas import tpu as pltpu
from jax.sharding import PartitionSpec as P

H = 8192
S = 2048
P_SIZE = 4096
MOST = 3


two_pi = 2.0 * math.pi
radix = 128
headroom = 1.25
softness = 0.01
epsilon = 1e-06


def contract(form, left, right):
    return jnp.einsum(
        form, left, right, precision=lax.Precision.HIGH, preferred_element_type=jnp.float32
    )


def make_tables(frequency, in_len, length, offset, sign):
    accum = length // radix
    blocks = in_len // radix
    first = frequency[:, :accum] % accum
    inner_index = first[:, :, None] * jnp.arange(blocks, dtype=jnp.int32)[None, None, :] % accum
    inner_angle = sign * two_pi / accum * inner_index.astype(jnp.float32)
    column = (jnp.arange(radix, dtype=jnp.int32) + offset) % length
    outer_index = frequency[:, :, None] * column[None, None, :] % length
    outer_angle = sign * two_pi / length * outer_index.astype(jnp.float32)
    shape_four = (frequency.shape[0], frequency.shape[1] // accum, accum, radix)
    return lax.optimization_barrier(
        (
            jnp.cos(inner_angle),
            jnp.sin(inner_angle),
            jnp.cos(outer_angle).reshape(shape_four),
            jnp.sin(outer_angle).reshape(shape_four),
        )
    )


def transform(real_part, imag_part, tables):
    inner_cos, inner_sin, outer_cos, outer_sin = tables
    batch, rows, width = real_part.shape
    blocks = width // radix
    real_four = real_part.reshape(batch, rows, blocks, radix)
    mid_real = contract("kpa,krab->krpb", inner_cos, real_four)
    mid_imag = contract("kpa,krab->krpb", inner_sin, real_four)
    if imag_part is not None:
        imag_four = imag_part.reshape(batch, rows, blocks, radix)
        mid_real = mid_real - contract("kpa,krab->krpb", inner_sin, imag_four)
        mid_imag = mid_imag + contract("kpa,krab->krpb", inner_cos, imag_four)
    return finish(mid_real, mid_imag, tables)


def finish(mid_real, mid_imag, tables):
    inner_cos, inner_sin, outer_cos, outer_sin = tables
    batch, rows = mid_real.shape[:2]
    out_real = contract("kqpb,krpb->krqp", outer_cos, mid_real) - contract(
        "kqpb,krpb->krqp", outer_sin, mid_imag
    )
    out_imag = contract("kqpb,krpb->krqp", outer_cos, mid_imag) + contract(
        "kqpb,krpb->krqp", outer_sin, mid_real
    )
    count = outer_cos.shape[1] * outer_cos.shape[2]
    return (out_real.reshape(batch, rows, count), out_imag.reshape(batch, rows, count))


def encode(field_real, field_imag, peak):
    scale = headroom * peak + epsilon
    unit_real = field_real / scale
    unit_imag = field_imag / scale
    square = unit_real * unit_real + unit_imag * unit_imag
    height = jnp.sqrt(1.0 - square)
    spread = jnp.sqrt(square + softness)
    phase_real = unit_real / spread
    phase_imag = unit_imag / spread
    plus_real = unit_real - phase_imag * height
    plus_imag = unit_imag + phase_real * height
    minus_real = unit_real + phase_imag * height
    minus_imag = unit_imag - phase_real * height
    return (plus_real, plus_imag, minus_real, minus_imag)


def body(holograms, sideband_centre, strip_owner):
    holo_count = holograms.shape[0]
    row_devices = lax.axis_size("row")
    col_devices = lax.axis_size("col")
    devices = row_devices * col_devices
    half = S // 2
    offsets = jnp.arange(S, dtype=jnp.int32) - half
    along_u = (sideband_centre[:, 0:1] + offsets[None, :]) % H
    along_v = (sideband_centre[:, 1:2] + offsets[None, :]) % H
    table_v = make_tables(along_v, H, H, 0, -1.0)
    table_u = make_tables(along_u, H, H, 0, -1.0)
    pixels = jnp.broadcast_to(jnp.arange(P_SIZE, dtype=jnp.int32)[None, :], (holo_count, P_SIZE))
    table_p = make_tables(pixels, S, P_SIZE, P_SIZE - half, 1.0)
    local_rows = holograms.shape[1]
    local_cols = holograms.shape[2]
    blocks = holograms.reshape(holo_count, col_devices, local_rows // col_devices, local_cols)
    piece = lax.all_to_all(blocks, "col", split_axis=1, concat_axis=1, tiled=True)
    lead, senders, count, width = piece.shape
    single = 1
    sender_blocks = width // radix
    piece_five = piece.reshape(lead, senders, count, sender_blocks, radix)
    inner_cos, inner_sin = table_v[0], table_v[1]
    per_sender = inner_cos.shape[:2] + (senders, sender_blocks)
    mid_real = contract("kpjc,kjrcb->krpb", inner_cos.reshape(per_sender), piece_five)
    mid_imag = contract("kpjc,kjrcb->krpb", inner_sin.reshape(per_sender), piece_five)
    share = S // devices
    outer_cos, outer_sin = table_v[2], table_v[3]
    form = "kqpb,krpb->qpkr"
    spec_real = contract(form, outer_cos, mid_real) - contract(form, outer_sin, mid_imag)
    spec_imag = contract(form, outer_cos, mid_imag) + contract(form, outer_sin, mid_real)
    send_shape = (devices, share, holo_count, count)
    piece_real = lax.all_to_all(spec_real.reshape(send_shape), ("row", "col"), 0, 0, tiled=True)
    piece_imag = lax.all_to_all(spec_imag.reshape(send_shape), ("row", "col"), 0, 0, tiled=True)
    pair = radix // count
    col_blocks = devices // pair
    recv_shape = (col_blocks, pair, share, holo_count, count)
    recv_real = piece_real.reshape(recv_shape)
    recv_imag = piece_imag.reshape(recv_shape)
    inner_cos, inner_sin = table_u[0], table_u[1]
    step = "kpa,alskr->ksplr"
    mid_real = contract(step, inner_cos, recv_real) - contract(step, inner_sin, recv_imag)
    mid_imag = contract(step, inner_sin, recv_real) + contract(step, inner_cos, recv_imag)
    mid_shape = (holo_count, share, inner_cos.shape[1], radix)
    side_real, side_imag = finish(mid_real.reshape(mid_shape), mid_imag.reshape(mid_shape), table_u)
    lift_real, lift_imag = transform(
        side_real.reshape(holo_count, share, S), side_imag.reshape(holo_count, share, S), table_p
    )
    strips = strip_owner.shape[0]
    strip_rows = P_SIZE // strips
    slot_rows = MOST * strip_rows
    strip_ids = jnp.arange(strips, dtype=jnp.int32)
    same = strip_owner[:, None] == strip_owner[None, :]
    before = strip_ids[None, :] < strip_ids[:, None]
    rank = jnp.sum((same & before).astype(jnp.int32), axis=1)
    slot_of = strip_owner * MOST + rank
    slot_ids = jnp.arange(strips * MOST, dtype=jnp.int32)
    match = slot_of[None, :] == slot_ids[:, None]
    source = jnp.sum(jnp.where(match, strip_ids[None, :], 0), axis=1)
    filled = jnp.any(match, axis=1).astype(jnp.float32)

    def pack(part):
        grouped = part.reshape(holo_count, share, strips, strip_rows)
        picked = jnp.take(grouped, source, axis=2) * filled[None, None, :, None]
        return jnp.transpose(picked.reshape(holo_count, share, strips, slot_rows), (2, 0, 1, 3))

    send_real = pack(lift_real)
    send_imag = pack(lift_imag)
    piece_real = lax.all_to_all(send_real, ("row", "col"), split_axis=0, concat_axis=2, tiled=True)
    piece_imag = lax.all_to_all(send_imag, ("row", "col"), split_axis=0, concat_axis=2, tiled=True)
    single, lead, width, count = piece_real.shape
    rows_real = jnp.swapaxes(piece_real.reshape(lead, width, count), 1, 2)
    rows_imag = jnp.swapaxes(piece_imag.reshape(lead, width, count), 1, 2)
    out_real, out_imag = transform(rows_real, rows_imag, table_p)
    field_real = out_real.reshape(single, lead, count, P_SIZE)
    field_imag = out_imag.reshape(single, lead, count, P_SIZE)
    field_real = field_real.reshape(holo_count, slot_rows, P_SIZE)
    field_imag = field_imag.reshape(holo_count, slot_rows, P_SIZE)
    magnitude = jnp.sqrt(field_real * field_real + field_imag * field_imag)
    local_peak = jnp.max(magnitude, axis=(1, 2))
    every = jnp.broadcast_to(local_peak[None, :], (devices, holo_count))
    peak = jnp.max(lax.all_to_all(every, ("row", "col"), 0, 0, tiled=True), axis=0)
    device_index = lax.axis_index("row") * col_devices + lax.axis_index("col")
    my_source = lax.dynamic_slice_in_dim(source, device_index * MOST, MOST)
    row_number = (
        my_source[:, None] * strip_rows + jnp.arange(strip_rows, dtype=jnp.int32)[None, :]
    ).reshape(slot_rows)
    parity = (row_number % 2)[:, None]
    return encode_slots(peak, parity, field_real, field_imag)


def encode_kernel(peak_ref, parity_ref, real_ref, imag_ref, out_ref):
    inverse = 1.0 / (headroom * peak_ref[pl.program_id(0)] + epsilon)
    unit_real = real_ref[0] * inverse
    unit_imag = imag_ref[0] * inverse
    square = unit_real * unit_real + unit_imag * unit_imag
    height = jnp.sqrt(1.0 - square)
    shrink = lax.rsqrt(square + softness) * height
    phase_real = unit_real * shrink
    phase_imag = unit_imag * shrink
    plus_real = unit_real - phase_imag
    plus_imag = unit_imag + phase_real
    minus_real = unit_real + phase_imag
    minus_imag = unit_imag - phase_real
    column = lax.broadcasted_iota(jnp.int32, plus_real.shape, 1)
    even = (parity_ref[...] + column) % 2 == 0
    out_ref[0, 0] = jnp.where(even, plus_real, minus_real)
    out_ref[0, 1] = jnp.where(even, plus_imag, minus_imag)


def encode_slots(peak, parity, field_real, field_imag):
    holo_count, rows, width = field_real.shape
    split = 2 if rows % 16 == 0 else 1
    block = rows // split
    field_spec = pl.BlockSpec((1, block, width), lambda k, j: (k, j, 0))
    return pl.pallas_call(
        encode_kernel,
        out_shape=jax.ShapeDtypeStruct((holo_count, 2, rows, width), jnp.float32),
        grid=(holo_count, split),
        in_specs=[
            pl.BlockSpec(memory_space=pltpu.SMEM),
            pl.BlockSpec((block, 1), lambda k, j: (j, 0)),
            field_spec,
            field_spec,
        ],
        out_specs=pl.BlockSpec((1, 2, block, width), lambda k, j: (k, 0, j, 0)),
    )(peak, parity, field_real, field_imag)


def solution(mesh):
    placed = (P(None, "row", "col"), P(), P())
    return jax.shard_map(
        body,
        mesh=mesh,
        in_specs=placed,
        out_specs=P(None, None, ("row", "col"), None),
        check_vma=False,
    )
```

```python
import math

import jax
import jax.numpy as jnp
from jax import lax
from jax.experimental import pallas as pl
from jax.experimental.pallas import tpu as pltpu
from jax.sharding import PartitionSpec as P

H = 8192
S = 2048
P_SIZE = 4096
MOST = 3


two_pi = 2.0 * math.pi
radix = 128
headroom = 1.25
softness = 0.01
epsilon = 1e-06


def contract(form, left, right):
    return jnp.einsum(
        form, left, right, precision=lax.Precision.HIGH, preferred_element_type=jnp.float32
    )


def make_tables(frequency, in_len, length, offset, sign):
    accum = length // radix
    blocks = in_len // radix
    first = frequency[:, :accum] % accum
    inner_index = first[:, :, None] * jnp.arange(blocks, dtype=jnp.int32)[None, None, :] % accum
    inner_angle = sign * two_pi / accum * inner_index.astype(jnp.float32)
    column = (jnp.arange(radix, dtype=jnp.int32) + offset) % length
    outer_index = frequency[:, :, None] * column[None, None, :] % length
    outer_angle = sign * two_pi / length * outer_index.astype(jnp.float32)
    shape_four = (frequency.shape[0], frequency.shape[1] // accum, accum, radix)
    return lax.optimization_barrier(
        (
            jnp.cos(inner_angle),
            jnp.sin(inner_angle),
            jnp.cos(outer_angle).reshape(shape_four),
            jnp.sin(outer_angle).reshape(shape_four),
        )
    )


def transform(real_part, imag_part, tables):
    inner_cos, inner_sin, outer_cos, outer_sin = tables
    batch, rows, width = real_part.shape
    blocks = width // radix
    real_four = real_part.reshape(batch, rows, blocks, radix)
    mid_real = contract("kpa,krab->krpb", inner_cos, real_four)
    mid_imag = contract("kpa,krab->krpb", inner_sin, real_four)
    if imag_part is not None:
        imag_four = imag_part.reshape(batch, rows, blocks, radix)
        mid_real = mid_real - contract("kpa,krab->krpb", inner_sin, imag_four)
        mid_imag = mid_imag + contract("kpa,krab->krpb", inner_cos, imag_four)
    return finish(mid_real, mid_imag, tables)


def finish(mid_real, mid_imag, tables):
    inner_cos, inner_sin, outer_cos, outer_sin = tables
    batch, rows = mid_real.shape[:2]
    out_real = contract("kqpb,krpb->krqp", outer_cos, mid_real) - contract(
        "kqpb,krpb->krqp", outer_sin, mid_imag
    )
    out_imag = contract("kqpb,krpb->krqp", outer_cos, mid_imag) + contract(
        "kqpb,krpb->krqp", outer_sin, mid_real
    )
    count = outer_cos.shape[1] * outer_cos.shape[2]
    return (out_real.reshape(batch, rows, count), out_imag.reshape(batch, rows, count))


def encode(field_real, field_imag, peak):
    scale = headroom * peak + epsilon
    unit_real = field_real / scale
    unit_imag = field_imag / scale
    square = unit_real * unit_real + unit_imag * unit_imag
    height = jnp.sqrt(1.0 - square)
    spread = jnp.sqrt(square + softness)
    phase_real = unit_real / spread
    phase_imag = unit_imag / spread
    plus_real = unit_real - phase_imag * height
    plus_imag = unit_imag + phase_real * height
    minus_real = unit_real + phase_imag * height
    minus_imag = unit_imag - phase_real * height
    return (plus_real, plus_imag, minus_real, minus_imag)


def body(holograms, sideband_centre, strip_owner):
    holo_count = holograms.shape[0]
    row_devices = lax.axis_size("row")
    col_devices = lax.axis_size("col")
    devices = row_devices * col_devices
    half = S // 2
    offsets = jnp.arange(S, dtype=jnp.int32) - half
    along_u = (sideband_centre[:, 0:1] + offsets[None, :]) % H
    along_v = (sideband_centre[:, 1:2] + offsets[None, :]) % H
    table_v = make_tables(along_v, H, H, 0, -1.0)
    table_u = make_tables(along_u, H, H, 0, -1.0)
    pixels = jnp.broadcast_to(jnp.arange(P_SIZE, dtype=jnp.int32)[None, :], (holo_count, P_SIZE))
    table_p = make_tables(pixels, S, P_SIZE, P_SIZE - half, 1.0)
    local_rows = holograms.shape[1]
    local_cols = holograms.shape[2]
    blocks = holograms.reshape(holo_count, col_devices, local_rows // col_devices, local_cols)
    piece = lax.all_to_all(blocks, "col", split_axis=1, concat_axis=1, tiled=True)
    lead, senders, count, width = piece.shape
    single = 1
    sender_blocks = width // radix
    piece_five = piece.reshape(lead, senders, count, sender_blocks, radix)
    inner_cos, inner_sin = table_v[0], table_v[1]
    per_sender = inner_cos.shape[:2] + (senders, sender_blocks)
    mid_real = contract("kpjc,kjrcb->krpb", inner_cos.reshape(per_sender), piece_five)
    mid_imag = contract("kpjc,kjrcb->krpb", inner_sin.reshape(per_sender), piece_five)
    share = S // devices
    outer_cos, outer_sin = table_v[2], table_v[3]
    form = "kqpb,krpb->qpkr"
    spec_real = contract(form, outer_cos, mid_real) - contract(form, outer_sin, mid_imag)
    spec_imag = contract(form, outer_cos, mid_imag) + contract(form, outer_sin, mid_real)
    send_shape = (devices, share, holo_count, count)
    piece_real = lax.all_to_all(spec_real.reshape(send_shape), ("row", "col"), 0, 0, tiled=True)
    piece_imag = lax.all_to_all(spec_imag.reshape(send_shape), ("row", "col"), 0, 0, tiled=True)
    pair = radix // count
    col_blocks = devices // pair
    recv_shape = (col_blocks, pair, share, holo_count, count)
    recv_real = piece_real.reshape(recv_shape)
    recv_imag = piece_imag.reshape(recv_shape)
    inner_cos, inner_sin = table_u[0], table_u[1]
    step = "kpa,alskr->ksplr"
    mid_real = contract(step, inner_cos, recv_real) - contract(step, inner_sin, recv_imag)
    mid_imag = contract(step, inner_sin, recv_real) + contract(step, inner_cos, recv_imag)
    mid_shape = (holo_count, share, inner_cos.shape[1], radix)
    side_real, side_imag = finish(mid_real.reshape(mid_shape), mid_imag.reshape(mid_shape), table_u)
    lift_real, lift_imag = transform(
        side_real.reshape(holo_count, share, S), side_imag.reshape(holo_count, share, S), table_p
    )
    strips = strip_owner.shape[0]
    strip_rows = P_SIZE // strips
    slot_rows = MOST * strip_rows
    strip_ids = jnp.arange(strips, dtype=jnp.int32)
    same = strip_owner[:, None] == strip_owner[None, :]
    before = strip_ids[None, :] < strip_ids[:, None]
    rank = jnp.sum((same & before).astype(jnp.int32), axis=1)
    slot_of = strip_owner * MOST + rank
    slot_ids = jnp.arange(strips * MOST, dtype=jnp.int32)
    match = slot_of[None, :] == slot_ids[:, None]
    source = jnp.sum(jnp.where(match, strip_ids[None, :], 0), axis=1)
    filled = jnp.any(match, axis=1).astype(jnp.float32)

    def pack(part):
        grouped = part.reshape(holo_count, share, strips, strip_rows)
        picked = jnp.take(grouped, source, axis=2) * filled[None, None, :, None]
        return jnp.transpose(picked.reshape(holo_count, share, strips, slot_rows), (2, 0, 1, 3))

    send_real = pack(lift_real)
    send_imag = pack(lift_imag)
    piece_real = lax.all_to_all(send_real, ("row", "col"), split_axis=0, concat_axis=2, tiled=True)
    piece_imag = lax.all_to_all(send_imag, ("row", "col"), split_axis=0, concat_axis=2, tiled=True)
    single, lead, width, count = piece_real.shape
    rows_real = jnp.swapaxes(piece_real.reshape(lead, width, count), 1, 2)
    rows_imag = jnp.swapaxes(piece_imag.reshape(lead, width, count), 1, 2)
    out_real, out_imag = transform(rows_real, rows_imag, table_p)
    field_real = out_real.reshape(single, lead, count, P_SIZE)
    field_imag = out_imag.reshape(single, lead, count, P_SIZE)
    field_real = field_real.reshape(holo_count, slot_rows, P_SIZE)
    field_imag = field_imag.reshape(holo_count, slot_rows, P_SIZE)
    magnitude = jnp.sqrt(field_real * field_real + field_imag * field_imag)
    local_peak = jnp.max(magnitude, axis=(1, 2))
    every = jnp.broadcast_to(local_peak[None, :], (devices, holo_count))
    peak = jnp.max(lax.all_to_all(every, ("row", "col"), 0, 0, tiled=True), axis=0)
    device_index = lax.axis_index("row") * col_devices + lax.axis_index("col")
    my_source = lax.dynamic_slice_in_dim(source, device_index * MOST, MOST)
    row_number = (
        my_source[:, None] * strip_rows + jnp.arange(strip_rows, dtype=jnp.int32)[None, :]
    ).reshape(slot_rows)
    parity = (row_number % 2)[:, None]
    return encode_slots(peak, parity, field_real, field_imag)


def encode_kernel(peak_ref, parity_ref, real_ref, imag_ref, out_ref):
    inverse = 1.0 / (headroom * peak_ref[pl.program_id(0)] + epsilon)
    _, coarse, fine, rows = real_ref.shape
    unit_real = real_ref[0].reshape(coarse * fine, rows).T * inverse
    unit_imag = imag_ref[0].reshape(coarse * fine, rows).T * inverse
    square = unit_real * unit_real + unit_imag * unit_imag
    height = jnp.sqrt(1.0 - square)
    shrink = lax.rsqrt(square + softness) * height
    phase_real = unit_real * shrink
    phase_imag = unit_imag * shrink
    plus_real = unit_real - phase_imag
    plus_imag = unit_imag + phase_real
    minus_real = unit_real + phase_imag
    minus_imag = unit_imag - phase_real
    column = lax.broadcasted_iota(jnp.int32, plus_real.shape, 1)
    even = (parity_ref[...] + column) % 2 == 0
    out_ref[0, 0] = jnp.where(even, plus_real, minus_real)
    out_ref[0, 1] = jnp.where(even, plus_imag, minus_imag)


def encode_slots(peak, parity, field_real, field_imag):
    holo_count, rows, width = field_real.shape
    fine = P_SIZE // radix
    coarse = width // fine
    part = 16
    split = coarse // part
    field_spec = pl.BlockSpec((1, part, fine, rows), lambda k, j: (k, j, 0, 0))

    def coarse_major(field):
        return jnp.transpose(field.reshape(holo_count, rows, coarse, fine), (0, 2, 3, 1))

    return pl.pallas_call(
        encode_kernel,
        out_shape=jax.ShapeDtypeStruct((holo_count, 2, rows, width), jnp.float32),
        grid=(holo_count, split),
        in_specs=[
            pl.BlockSpec(memory_space=pltpu.SMEM),
            pl.BlockSpec((rows, 1), lambda k, j: (0, 0)),
            field_spec,
            field_spec,
        ],
        out_specs=pl.BlockSpec((1, 2, rows, part * fine), lambda k, j: (k, 0, 0, j)),
    )(peak, parity, coarse_major(field_real), coarse_major(field_imag))


def solution(mesh):
    placed = (P(None, "row", "col"), P(), P())
    return jax.shard_map(
        body,
        mesh=mesh,
        in_specs=placed,
        out_specs=P(None, None, ("row", "col"), None),
        check_vma=False,
    )
```

```python
import math

import jax
import jax.numpy as jnp
from jax import lax
from jax.experimental import pallas as pl
from jax.experimental.pallas import tpu as pltpu
from jax.sharding import PartitionSpec as P

H = 8192
S = 2048
P_SIZE = 4096
MOST = 3


two_pi = 2.0 * math.pi
radix = 128
headroom = 1.25
softness = 0.01
epsilon = 1e-06


def contract(form, left, right):
    return jnp.einsum(
        form, left, right, precision=lax.Precision.HIGH, preferred_element_type=jnp.float32
    )


def make_tables(frequency, in_len, length, offset, sign):
    accum = length // radix
    blocks = in_len // radix
    first = frequency[:, :accum] % accum
    inner_index = first[:, :, None] * jnp.arange(blocks, dtype=jnp.int32)[None, None, :] % accum
    inner_angle = sign * two_pi / accum * inner_index.astype(jnp.float32)
    column = (jnp.arange(radix, dtype=jnp.int32) + offset) % length
    outer_index = frequency[:, :, None] * column[None, None, :] % length
    outer_angle = sign * two_pi / length * outer_index.astype(jnp.float32)
    shape_four = (frequency.shape[0], frequency.shape[1] // accum, accum, radix)
    return lax.optimization_barrier(
        (
            jnp.cos(inner_angle),
            jnp.sin(inner_angle),
            jnp.cos(outer_angle).reshape(shape_four),
            jnp.sin(outer_angle).reshape(shape_four),
        )
    )


def transform(real_part, imag_part, tables):
    inner_cos, inner_sin, outer_cos, outer_sin = tables
    batch, rows, width = real_part.shape
    blocks = width // radix
    real_four = real_part.reshape(batch, rows, blocks, radix)
    mid_real = contract("kpa,krab->krpb", inner_cos, real_four)
    mid_imag = contract("kpa,krab->krpb", inner_sin, real_four)
    if imag_part is not None:
        imag_four = imag_part.reshape(batch, rows, blocks, radix)
        mid_real = mid_real - contract("kpa,krab->krpb", inner_sin, imag_four)
        mid_imag = mid_imag + contract("kpa,krab->krpb", inner_cos, imag_four)
    return finish(mid_real, mid_imag, tables)


def finish(mid_real, mid_imag, tables):
    inner_cos, inner_sin, outer_cos, outer_sin = tables
    batch, rows = mid_real.shape[:2]
    out_real = contract("kqpb,krpb->krqp", outer_cos, mid_real) - contract(
        "kqpb,krpb->krqp", outer_sin, mid_imag
    )
    out_imag = contract("kqpb,krpb->krqp", outer_cos, mid_imag) + contract(
        "kqpb,krpb->krqp", outer_sin, mid_real
    )
    count = outer_cos.shape[1] * outer_cos.shape[2]
    return (out_real.reshape(batch, rows, count), out_imag.reshape(batch, rows, count))


def encode(field_real, field_imag, peak):
    scale = headroom * peak + epsilon
    unit_real = field_real / scale
    unit_imag = field_imag / scale
    square = unit_real * unit_real + unit_imag * unit_imag
    height = jnp.sqrt(1.0 - square)
    spread = jnp.sqrt(square + softness)
    phase_real = unit_real / spread
    phase_imag = unit_imag / spread
    plus_real = unit_real - phase_imag * height
    plus_imag = unit_imag + phase_real * height
    minus_real = unit_real + phase_imag * height
    minus_imag = unit_imag - phase_real * height
    return (plus_real, plus_imag, minus_real, minus_imag)


def body(holograms, sideband_centre, strip_owner):
    holo_count = holograms.shape[0]
    row_devices = lax.axis_size("row")
    col_devices = lax.axis_size("col")
    devices = row_devices * col_devices
    half = S // 2
    offsets = jnp.arange(S, dtype=jnp.int32) - half
    along_u = (sideband_centre[:, 0:1] + offsets[None, :]) % H
    along_v = (sideband_centre[:, 1:2] + offsets[None, :]) % H
    table_v = make_tables(along_v, H, H, 0, -1.0)
    table_u = make_tables(along_u, H, H, 0, -1.0)
    pixels = jnp.broadcast_to(jnp.arange(P_SIZE, dtype=jnp.int32)[None, :], (holo_count, P_SIZE))
    table_p = make_tables(pixels, S, P_SIZE, P_SIZE - half, 1.0)
    local_rows = holograms.shape[1]
    local_cols = holograms.shape[2]
    blocks = holograms.reshape(holo_count, col_devices, local_rows // col_devices, local_cols)
    piece = lax.all_to_all(blocks, "col", split_axis=1, concat_axis=1, tiled=True)
    lead, senders, count, width = piece.shape
    single = 1
    sender_blocks = width // radix
    piece_five = piece.reshape(lead, senders, count, sender_blocks, radix)
    inner_cos, inner_sin = table_v[0], table_v[1]
    per_sender = inner_cos.shape[:2] + (senders, sender_blocks)
    mid_real = contract("kpjc,kjrcb->krpb", inner_cos.reshape(per_sender), piece_five)
    mid_imag = contract("kpjc,kjrcb->krpb", inner_sin.reshape(per_sender), piece_five)
    share = S // devices
    outer_cos, outer_sin = table_v[2], table_v[3]
    form = "kqpb,krpb->qpkr"
    spec_real = contract(form, outer_cos, mid_real) - contract(form, outer_sin, mid_imag)
    spec_imag = contract(form, outer_cos, mid_imag) + contract(form, outer_sin, mid_real)
    send_shape = (devices, share, holo_count, count)
    piece_real = lax.all_to_all(spec_real.reshape(send_shape), ("row", "col"), 0, 0, tiled=True)
    piece_imag = lax.all_to_all(spec_imag.reshape(send_shape), ("row", "col"), 0, 0, tiled=True)
    pair = radix // count
    col_blocks = devices // pair
    recv_shape = (col_blocks, pair, share, holo_count, count)
    recv_real = piece_real.reshape(recv_shape)
    recv_imag = piece_imag.reshape(recv_shape)
    inner_cos, inner_sin = table_u[0], table_u[1]
    step = "kpa,alskr->ksplr"
    mid_real = contract(step, inner_cos, recv_real) - contract(step, inner_sin, recv_imag)
    mid_imag = contract(step, inner_sin, recv_real) + contract(step, inner_cos, recv_imag)
    mid_shape = (holo_count, share, inner_cos.shape[1], radix)
    side_real, side_imag = finish(mid_real.reshape(mid_shape), mid_imag.reshape(mid_shape), table_u)
    lift_real, lift_imag = transform(
        side_real.reshape(holo_count, share, S), side_imag.reshape(holo_count, share, S), table_p
    )
    strips = strip_owner.shape[0]
    strip_rows = P_SIZE // strips
    slot_rows = MOST * strip_rows
    strip_ids = jnp.arange(strips, dtype=jnp.int32)
    same = strip_owner[:, None] == strip_owner[None, :]
    before = strip_ids[None, :] < strip_ids[:, None]
    rank = jnp.sum((same & before).astype(jnp.int32), axis=1)
    slot_of = strip_owner * MOST + rank
    slot_ids = jnp.arange(strips * MOST, dtype=jnp.int32)
    match = slot_of[None, :] == slot_ids[:, None]
    source = jnp.sum(jnp.where(match, strip_ids[None, :], 0), axis=1)
    filled = jnp.any(match, axis=1).astype(jnp.float32)

    def pack(part):
        grouped = part.reshape(holo_count, share, strips, strip_rows)
        picked = jnp.take(grouped, source, axis=2) * filled[None, None, :, None]
        return jnp.transpose(picked.reshape(holo_count, share, strips, slot_rows), (2, 0, 1, 3))

    send_real = pack(lift_real)
    send_imag = pack(lift_imag)
    dense = (devices, 1, holo_count * share * slot_rows)
    piece_real = lax.all_to_all(send_real.reshape(dense), ("row", "col"), 0, 0, tiled=True)
    piece_imag = lax.all_to_all(send_imag.reshape(dense), ("row", "col"), 0, 0, tiled=True)

    def unpack(piece):
        piece = piece.reshape(devices, holo_count, share, slot_rows)
        return jnp.transpose(piece, (1, 3, 0, 2)).reshape(holo_count, slot_rows, devices * share)

    rows_real = unpack(piece_real)
    rows_imag = unpack(piece_imag)
    out_real, out_imag = transform(rows_real, rows_imag, table_p)
    field_real = out_real.reshape(holo_count, slot_rows, P_SIZE)
    field_imag = out_imag.reshape(holo_count, slot_rows, P_SIZE)
    magnitude = jnp.sqrt(field_real * field_real + field_imag * field_imag)
    local_peak = jnp.max(magnitude, axis=(1, 2))
    every = jnp.broadcast_to(local_peak[None, :], (devices, holo_count))
    peak = jnp.max(lax.all_to_all(every, ("row", "col"), 0, 0, tiled=True), axis=0)
    device_index = lax.axis_index("row") * col_devices + lax.axis_index("col")
    my_source = lax.dynamic_slice_in_dim(source, device_index * MOST, MOST)
    row_number = (
        my_source[:, None] * strip_rows + jnp.arange(strip_rows, dtype=jnp.int32)[None, :]
    ).reshape(slot_rows)
    parity = (row_number % 2)[:, None]
    return encode_slots(peak, parity, field_real, field_imag)


def encode_kernel(peak_ref, parity_ref, real_ref, imag_ref, out_ref):
    inverse = 1.0 / (headroom * peak_ref[pl.program_id(0)] + epsilon)
    unit_real = real_ref[0] * inverse
    unit_imag = imag_ref[0] * inverse
    square = unit_real * unit_real + unit_imag * unit_imag
    height = jnp.sqrt(1.0 - square)
    shrink = lax.rsqrt(square + softness) * height
    phase_real = unit_real * shrink
    phase_imag = unit_imag * shrink
    plus_real = unit_real - phase_imag
    plus_imag = unit_imag + phase_real
    minus_real = unit_real + phase_imag
    minus_imag = unit_imag - phase_real
    column = lax.broadcasted_iota(jnp.int32, plus_real.shape, 1)
    even = (parity_ref[...] + column) % 2 == 0
    out_ref[0, 0] = jnp.where(even, plus_real, minus_real)
    out_ref[0, 1] = jnp.where(even, plus_imag, minus_imag)


def encode_slots(peak, parity, field_real, field_imag):
    holo_count, rows, width = field_real.shape
    split = 2 if rows % 16 == 0 else 1
    block = rows // split
    field_spec = pl.BlockSpec((1, block, width), lambda k, j: (k, j, 0))
    return pl.pallas_call(
        encode_kernel,
        out_shape=jax.ShapeDtypeStruct((holo_count, 2, rows, width), jnp.float32),
        grid=(holo_count, split),
        in_specs=[
            pl.BlockSpec(memory_space=pltpu.SMEM),
            pl.BlockSpec((block, 1), lambda k, j: (j, 0)),
            field_spec,
            field_spec,
        ],
        out_specs=pl.BlockSpec((1, 2, block, width), lambda k, j: (k, 0, j, 0)),
    )(peak, parity, field_real, field_imag)


def solution(mesh):
    placed = (P(None, "row", "col"), P(), P())
    return jax.shard_map(
        body,
        mesh=mesh,
        in_specs=placed,
        out_specs=P(None, None, ("row", "col"), None),
        check_vma=False,
    )
```

```python
import math

import jax
import jax.numpy as jnp
from jax import lax
from jax.experimental import pallas as pl
from jax.experimental.pallas import tpu as pltpu
from jax.sharding import PartitionSpec as P

H = 8192
S = 2048
P_SIZE = 4096
MOST = 3


two_pi = 2.0 * math.pi
radix = 128
headroom = 1.25
softness = 0.01
epsilon = 1e-06


def contract(form, left, right):
    return jnp.einsum(
        form, left, right, precision=lax.Precision.HIGH, preferred_element_type=jnp.float32
    )


def make_tables(frequency, in_len, length, offset, sign):
    accum = length // radix
    blocks = in_len // radix
    first = frequency[:, :accum] % accum
    inner_index = first[:, :, None] * jnp.arange(blocks, dtype=jnp.int32)[None, None, :] % accum
    inner_angle = sign * two_pi / accum * inner_index.astype(jnp.float32)
    column = (jnp.arange(radix, dtype=jnp.int32) + offset) % length
    outer_index = frequency[:, :, None] * column[None, None, :] % length
    outer_angle = sign * two_pi / length * outer_index.astype(jnp.float32)
    shape_four = (frequency.shape[0], frequency.shape[1] // accum, accum, radix)
    return lax.optimization_barrier(
        (
            jnp.cos(inner_angle),
            jnp.sin(inner_angle),
            jnp.cos(outer_angle).reshape(shape_four),
            jnp.sin(outer_angle).reshape(shape_four),
        )
    )


def transform(real_part, imag_part, tables):
    inner_cos, inner_sin, outer_cos, outer_sin = tables
    batch, rows, width = real_part.shape
    blocks = width // radix
    real_four = real_part.reshape(batch, rows, blocks, radix)
    mid_real = contract("kpa,krab->krpb", inner_cos, real_four)
    mid_imag = contract("kpa,krab->krpb", inner_sin, real_four)
    if imag_part is not None:
        imag_four = imag_part.reshape(batch, rows, blocks, radix)
        mid_real = mid_real - contract("kpa,krab->krpb", inner_sin, imag_four)
        mid_imag = mid_imag + contract("kpa,krab->krpb", inner_cos, imag_four)
    return finish(mid_real, mid_imag, tables)


def finish(mid_real, mid_imag, tables):
    inner_cos, inner_sin, outer_cos, outer_sin = tables
    batch, rows = mid_real.shape[:2]
    out_real = contract("kqpb,krpb->krqp", outer_cos, mid_real) - contract(
        "kqpb,krpb->krqp", outer_sin, mid_imag
    )
    out_imag = contract("kqpb,krpb->krqp", outer_cos, mid_imag) + contract(
        "kqpb,krpb->krqp", outer_sin, mid_real
    )
    count = outer_cos.shape[1] * outer_cos.shape[2]
    return (out_real.reshape(batch, rows, count), out_imag.reshape(batch, rows, count))


def encode(field_real, field_imag, peak):
    scale = headroom * peak + epsilon
    unit_real = field_real / scale
    unit_imag = field_imag / scale
    square = unit_real * unit_real + unit_imag * unit_imag
    height = jnp.sqrt(1.0 - square)
    spread = jnp.sqrt(square + softness)
    phase_real = unit_real / spread
    phase_imag = unit_imag / spread
    plus_real = unit_real - phase_imag * height
    plus_imag = unit_imag + phase_real * height
    minus_real = unit_real + phase_imag * height
    minus_imag = unit_imag - phase_real * height
    return (plus_real, plus_imag, minus_real, minus_imag)


def body(holograms, sideband_centre, strip_owner):
    holo_count = holograms.shape[0]
    row_devices = lax.axis_size("row")
    col_devices = lax.axis_size("col")
    devices = row_devices * col_devices
    half = S // 2
    offsets = jnp.arange(S, dtype=jnp.int32) - half
    along_u = (sideband_centre[:, 0:1] + offsets[None, :]) % H
    along_v = (sideband_centre[:, 1:2] + offsets[None, :]) % H
    table_v = make_tables(along_v, H, H, 0, -1.0)
    table_u = make_tables(along_u, H, H, 0, -1.0)
    pixels = jnp.broadcast_to(jnp.arange(P_SIZE, dtype=jnp.int32)[None, :], (holo_count, P_SIZE))
    table_p = make_tables(pixels, S, P_SIZE, P_SIZE - half, 1.0)
    local_rows = holograms.shape[1]
    local_cols = holograms.shape[2]
    blocks = holograms.reshape(holo_count, col_devices, local_rows // col_devices, local_cols)
    share = S // devices
    inner_cos, inner_sin, outer_cos, outer_sin = table_v
    form = "kqpb,krpb->qpkr"
    halves = 2
    half_rows = blocks.shape[2] // halves
    spec_parts = []
    for h in range(halves):
        part = blocks[:, :, h * half_rows : (h + 1) * half_rows]
        piece = lax.all_to_all(part, "col", split_axis=1, concat_axis=1, tiled=True)
        lead, senders, rows_here, width = piece.shape
        sender_blocks = width // radix
        piece_five = piece.reshape(lead, senders, rows_here, sender_blocks, radix)
        per_sender = inner_cos.shape[:2] + (senders, sender_blocks)
        mid_real = contract("kpjc,kjrcb->krpb", inner_cos.reshape(per_sender), piece_five)
        mid_imag = contract("kpjc,kjrcb->krpb", inner_sin.reshape(per_sender), piece_five)
        part_real = contract(form, outer_cos, mid_real) - contract(form, outer_sin, mid_imag)
        part_imag = contract(form, outer_cos, mid_imag) + contract(form, outer_sin, mid_real)
        spec_parts.append((part_real, part_imag))
    spec_real = jnp.concatenate([part[0] for part in spec_parts], axis=3)
    spec_imag = jnp.concatenate([part[1] for part in spec_parts], axis=3)
    count = spec_real.shape[3]
    send_shape = (devices, share, holo_count, count)
    piece_real = lax.all_to_all(spec_real.reshape(send_shape), ("row", "col"), 0, 0, tiled=True)
    piece_imag = lax.all_to_all(spec_imag.reshape(send_shape), ("row", "col"), 0, 0, tiled=True)
    pair = radix // count
    col_blocks = devices // pair
    recv_shape = (col_blocks, pair, share, holo_count, count)
    recv_real = piece_real.reshape(recv_shape)
    recv_imag = piece_imag.reshape(recv_shape)
    inner_cos, inner_sin = table_u[0], table_u[1]
    step = "kpa,alskr->ksplr"
    mid_real = contract(step, inner_cos, recv_real) - contract(step, inner_sin, recv_imag)
    mid_imag = contract(step, inner_sin, recv_real) + contract(step, inner_cos, recv_imag)
    mid_shape = (holo_count, share, inner_cos.shape[1], radix)
    side_real, side_imag = finish(mid_real.reshape(mid_shape), mid_imag.reshape(mid_shape), table_u)
    lift_real, lift_imag = transform(
        side_real.reshape(holo_count, share, S), side_imag.reshape(holo_count, share, S), table_p
    )
    strips = strip_owner.shape[0]
    strip_rows = P_SIZE // strips
    slot_rows = MOST * strip_rows
    strip_ids = jnp.arange(strips, dtype=jnp.int32)
    same = strip_owner[:, None] == strip_owner[None, :]
    before = strip_ids[None, :] < strip_ids[:, None]
    rank = jnp.sum((same & before).astype(jnp.int32), axis=1)
    slot_of = strip_owner * MOST + rank
    slot_ids = jnp.arange(strips * MOST, dtype=jnp.int32)
    match = slot_of[None, :] == slot_ids[:, None]
    source = jnp.sum(jnp.where(match, strip_ids[None, :], 0), axis=1)
    filled = jnp.any(match, axis=1).astype(jnp.float32)

    def pack(part):
        grouped = part.reshape(holo_count, share, strips, strip_rows)
        picked = jnp.take(grouped, source, axis=2) * filled[None, None, :, None]
        return jnp.transpose(picked.reshape(holo_count, share, strips, slot_rows), (2, 0, 1, 3))

    send_real = pack(lift_real)
    send_imag = pack(lift_imag)
    dense = (devices, 1, holo_count * share * slot_rows)
    piece_real = lax.all_to_all(send_real.reshape(dense), ("row", "col"), 0, 0, tiled=True)
    piece_imag = lax.all_to_all(send_imag.reshape(dense), ("row", "col"), 0, 0, tiled=True)

    def unpack(piece):
        piece = piece.reshape(devices, holo_count, share, slot_rows)
        return jnp.transpose(piece, (1, 3, 0, 2)).reshape(holo_count, slot_rows, devices * share)

    rows_real = unpack(piece_real)
    rows_imag = unpack(piece_imag)
    out_real, out_imag = transform(rows_real, rows_imag, table_p)
    field_real = out_real.reshape(holo_count, slot_rows, P_SIZE)
    field_imag = out_imag.reshape(holo_count, slot_rows, P_SIZE)
    magnitude = jnp.sqrt(field_real * field_real + field_imag * field_imag)
    local_peak = jnp.max(magnitude, axis=(1, 2))
    every = jnp.broadcast_to(local_peak[None, :], (devices, holo_count))
    peak = jnp.max(lax.all_to_all(every, ("row", "col"), 0, 0, tiled=True), axis=0)
    device_index = lax.axis_index("row") * col_devices + lax.axis_index("col")
    my_source = lax.dynamic_slice_in_dim(source, device_index * MOST, MOST)
    row_number = (
        my_source[:, None] * strip_rows + jnp.arange(strip_rows, dtype=jnp.int32)[None, :]
    ).reshape(slot_rows)
    parity = (row_number % 2)[:, None]
    return encode_slots(peak, parity, field_real, field_imag)


def encode_kernel(peak_ref, parity_ref, real_ref, imag_ref, out_ref):
    inverse = 1.0 / (headroom * peak_ref[pl.program_id(0)] + epsilon)
    unit_real = real_ref[0] * inverse
    unit_imag = imag_ref[0] * inverse
    square = unit_real * unit_real + unit_imag * unit_imag
    height = jnp.sqrt(1.0 - square)
    shrink = lax.rsqrt(square + softness) * height
    phase_real = unit_real * shrink
    phase_imag = unit_imag * shrink
    plus_real = unit_real - phase_imag
    plus_imag = unit_imag + phase_real
    minus_real = unit_real + phase_imag
    minus_imag = unit_imag - phase_real
    column = lax.broadcasted_iota(jnp.int32, plus_real.shape, 1)
    even = (parity_ref[...] + column) % 2 == 0
    out_ref[0, 0] = jnp.where(even, plus_real, minus_real)
    out_ref[0, 1] = jnp.where(even, plus_imag, minus_imag)


def encode_slots(peak, parity, field_real, field_imag):
    holo_count, rows, width = field_real.shape
    split = 2 if rows % 16 == 0 else 1
    block = rows // split
    field_spec = pl.BlockSpec((1, block, width), lambda k, j: (k, j, 0))
    return pl.pallas_call(
        encode_kernel,
        out_shape=jax.ShapeDtypeStruct((holo_count, 2, rows, width), jnp.float32),
        grid=(holo_count, split),
        in_specs=[
            pl.BlockSpec(memory_space=pltpu.SMEM),
            pl.BlockSpec((block, 1), lambda k, j: (j, 0)),
            field_spec,
            field_spec,
        ],
        out_specs=pl.BlockSpec((1, 2, block, width), lambda k, j: (k, 0, j, 0)),
    )(peak, parity, field_real, field_imag)


def solution(mesh):
    placed = (P(None, "row", "col"), P(), P())
    return jax.shard_map(
        body,
        mesh=mesh,
        in_specs=placed,
        out_specs=P(None, None, ("row", "col"), None),
        check_vma=False,
    )
```

```python
import math

import jax
import jax.numpy as jnp
from jax import lax
from jax.experimental import pallas as pl
from jax.experimental.pallas import tpu as pltpu
from jax.sharding import PartitionSpec as P

H = 8192
S = 2048
P_SIZE = 4096
MOST = 3


two_pi = 2.0 * math.pi
radix = 128
headroom = 1.25
softness = 0.01
epsilon = 1e-06


def contract(form, left, right):
    return jnp.einsum(
        form, left, right, precision=lax.Precision.HIGH, preferred_element_type=jnp.float32
    )


def make_tables(frequency, in_len, length, offset, sign):
    accum = length // radix
    blocks = in_len // radix
    first = frequency[:, :accum] % accum
    inner_index = first[:, :, None] * jnp.arange(blocks, dtype=jnp.int32)[None, None, :] % accum
    inner_angle = sign * two_pi / accum * inner_index.astype(jnp.float32)
    column = (jnp.arange(radix, dtype=jnp.int32) + offset) % length
    outer_index = frequency[:, :, None] * column[None, None, :] % length
    outer_angle = sign * two_pi / length * outer_index.astype(jnp.float32)
    shape_four = (frequency.shape[0], frequency.shape[1] // accum, accum, radix)
    return lax.optimization_barrier(
        (
            jnp.cos(inner_angle),
            jnp.sin(inner_angle),
            jnp.cos(outer_angle).reshape(shape_four),
            jnp.sin(outer_angle).reshape(shape_four),
        )
    )


def transform(real_part, imag_part, tables):
    inner_cos, inner_sin, outer_cos, outer_sin = tables
    batch, rows, width = real_part.shape
    blocks = width // radix
    real_four = real_part.reshape(batch, rows, blocks, radix)
    mid_real = contract("kpa,krab->krpb", inner_cos, real_four)
    mid_imag = contract("kpa,krab->krpb", inner_sin, real_four)
    if imag_part is not None:
        imag_four = imag_part.reshape(batch, rows, blocks, radix)
        mid_real = mid_real - contract("kpa,krab->krpb", inner_sin, imag_four)
        mid_imag = mid_imag + contract("kpa,krab->krpb", inner_cos, imag_four)
    return finish(mid_real, mid_imag, tables)


def finish(mid_real, mid_imag, tables):
    inner_cos, inner_sin, outer_cos, outer_sin = tables
    batch, rows = mid_real.shape[:2]
    out_real = contract("kqpb,krpb->krqp", outer_cos, mid_real) - contract(
        "kqpb,krpb->krqp", outer_sin, mid_imag
    )
    out_imag = contract("kqpb,krpb->krqp", outer_cos, mid_imag) + contract(
        "kqpb,krpb->krqp", outer_sin, mid_real
    )
    count = outer_cos.shape[1] * outer_cos.shape[2]
    return (out_real.reshape(batch, rows, count), out_imag.reshape(batch, rows, count))


def encode(field_real, field_imag, peak):
    scale = headroom * peak + epsilon
    unit_real = field_real / scale
    unit_imag = field_imag / scale
    square = unit_real * unit_real + unit_imag * unit_imag
    height = jnp.sqrt(1.0 - square)
    spread = jnp.sqrt(square + softness)
    phase_real = unit_real / spread
    phase_imag = unit_imag / spread
    plus_real = unit_real - phase_imag * height
    plus_imag = unit_imag + phase_real * height
    minus_real = unit_real + phase_imag * height
    minus_imag = unit_imag - phase_real * height
    return (plus_real, plus_imag, minus_real, minus_imag)


def body(holograms, sideband_centre, strip_owner):
    holo_count = holograms.shape[0]
    row_devices = lax.axis_size("row")
    col_devices = lax.axis_size("col")
    devices = row_devices * col_devices
    half = S // 2
    offsets = jnp.arange(S, dtype=jnp.int32) - half
    along_u = (sideband_centre[:, 0:1] + offsets[None, :]) % H
    along_v = (sideband_centre[:, 1:2] + offsets[None, :]) % H
    table_v = make_tables(along_v, H, H, 0, -1.0)
    table_u = make_tables(along_u, H, H, 0, -1.0)
    pixels = jnp.broadcast_to(jnp.arange(P_SIZE, dtype=jnp.int32)[None, :], (holo_count, P_SIZE))
    table_p = make_tables(pixels, S, P_SIZE, P_SIZE - half, 1.0)
    local_rows = holograms.shape[1]
    local_cols = holograms.shape[2]
    blocks = holograms.reshape(holo_count, col_devices, local_rows // col_devices, local_cols)
    piece = lax.all_to_all(blocks, "col", split_axis=1, concat_axis=1, tiled=True)
    lead, senders, count, width = piece.shape
    single = 1
    sender_blocks = width // radix
    piece_five = piece.reshape(lead, senders, count, sender_blocks, radix)
    inner_cos, inner_sin = table_v[0], table_v[1]
    per_sender = inner_cos.shape[:2] + (senders, sender_blocks)
    mid_real = contract("kpjc,kjrcb->krpb", inner_cos.reshape(per_sender), piece_five)
    mid_imag = contract("kpjc,kjrcb->krpb", inner_sin.reshape(per_sender), piece_five)
    share = S // devices
    outer_cos, outer_sin = table_v[2], table_v[3]
    groups = outer_cos.shape[2] // share
    split_shape = outer_cos.shape[:2] + (groups, share, radix)
    outer_cos = outer_cos.reshape(split_shape)
    outer_sin = outer_sin.reshape(split_shape)
    mid_real = mid_real.reshape(mid_real.shape[:2] + (groups, share, radix))
    mid_imag = mid_imag.reshape(mid_imag.shape[:2] + (groups, share, radix))
    form = "kqhsb,krhsb->qhksr"
    spec_real = contract(form, outer_cos, mid_real) - contract(form, outer_sin, mid_imag)
    spec_imag = contract(form, outer_cos, mid_imag) + contract(form, outer_sin, mid_real)
    send_shape = (devices, holo_count, share, count)
    piece_real = lax.all_to_all(spec_real.reshape(send_shape), ("row", "col"), 0, 0, tiled=True)
    piece_imag = lax.all_to_all(spec_imag.reshape(send_shape), ("row", "col"), 0, 0, tiled=True)
    pair = radix // count
    col_blocks = devices // pair
    recv_shape = (col_blocks, pair, holo_count, share, count)
    recv_real = piece_real.reshape(recv_shape)
    recv_imag = piece_imag.reshape(recv_shape)
    inner_cos, inner_sin = table_u[0], table_u[1]
    step = "kpa,alksr->ksplr"
    mid_real = contract(step, inner_cos, recv_real) - contract(step, inner_sin, recv_imag)
    mid_imag = contract(step, inner_sin, recv_real) + contract(step, inner_cos, recv_imag)
    mid_shape = (holo_count, share, inner_cos.shape[1], radix)
    side_real, side_imag = finish(mid_real.reshape(mid_shape), mid_imag.reshape(mid_shape), table_u)
    lift_real, lift_imag = transform(
        side_real.reshape(holo_count, share, S), side_imag.reshape(holo_count, share, S), table_p
    )
    strips = strip_owner.shape[0]
    strip_rows = P_SIZE // strips
    slot_rows = MOST * strip_rows
    strip_ids = jnp.arange(strips, dtype=jnp.int32)
    same = strip_owner[:, None] == strip_owner[None, :]
    before = strip_ids[None, :] < strip_ids[:, None]
    rank = jnp.sum((same & before).astype(jnp.int32), axis=1)
    slot_of = strip_owner * MOST + rank
    slot_ids = jnp.arange(strips * MOST, dtype=jnp.int32)
    match = slot_of[None, :] == slot_ids[:, None]
    source = jnp.sum(jnp.where(match, strip_ids[None, :], 0), axis=1)
    filled = jnp.any(match, axis=1).astype(jnp.float32)

    def pack(part):
        grouped = part.reshape(holo_count, share, strips, strip_rows)
        picked = jnp.take(grouped, source, axis=2) * filled[None, None, :, None]
        return jnp.transpose(picked.reshape(holo_count, share, strips, slot_rows), (2, 0, 1, 3))

    send_real = pack(lift_real)
    send_imag = pack(lift_imag)
    dense = (devices, 1, holo_count * share * slot_rows)
    piece_real = lax.all_to_all(send_real.reshape(dense), ("row", "col"), 0, 0, tiled=True)
    piece_imag = lax.all_to_all(send_imag.reshape(dense), ("row", "col"), 0, 0, tiled=True)

    def unpack(piece):
        piece = piece.reshape(devices, holo_count, share, slot_rows)
        return jnp.transpose(piece, (1, 3, 0, 2)).reshape(holo_count, slot_rows, devices * share)

    rows_real = unpack(piece_real)
    rows_imag = unpack(piece_imag)
    out_real, out_imag = transform(rows_real, rows_imag, table_p)
    field_real = out_real.reshape(holo_count, slot_rows, P_SIZE)
    field_imag = out_imag.reshape(holo_count, slot_rows, P_SIZE)
    magnitude = jnp.sqrt(field_real * field_real + field_imag * field_imag)
    local_peak = jnp.max(magnitude, axis=(1, 2))
    every = jnp.broadcast_to(local_peak[None, :], (devices, holo_count))
    peak = jnp.max(lax.all_to_all(every, ("row", "col"), 0, 0, tiled=True), axis=0)
    device_index = lax.axis_index("row") * col_devices + lax.axis_index("col")
    my_source = lax.dynamic_slice_in_dim(source, device_index * MOST, MOST)
    row_number = (
        my_source[:, None] * strip_rows + jnp.arange(strip_rows, dtype=jnp.int32)[None, :]
    ).reshape(slot_rows)
    parity = (row_number % 2)[:, None]
    return encode_slots(peak, parity, field_real, field_imag)


def encode_kernel(peak_ref, parity_ref, real_ref, imag_ref, out_ref):
    inverse = 1.0 / (headroom * peak_ref[pl.program_id(0)] + epsilon)
    unit_real = real_ref[0] * inverse
    unit_imag = imag_ref[0] * inverse
    square = unit_real * unit_real + unit_imag * unit_imag
    height = jnp.sqrt(1.0 - square)
    shrink = lax.rsqrt(square + softness) * height
    phase_real = unit_real * shrink
    phase_imag = unit_imag * shrink
    plus_real = unit_real - phase_imag
    plus_imag = unit_imag + phase_real
    minus_real = unit_real + phase_imag
    minus_imag = unit_imag - phase_real
    column = lax.broadcasted_iota(jnp.int32, plus_real.shape, 1)
    even = (parity_ref[...] + column) % 2 == 0
    out_ref[0, 0] = jnp.where(even, plus_real, minus_real)
    out_ref[0, 1] = jnp.where(even, plus_imag, minus_imag)


def encode_slots(peak, parity, field_real, field_imag):
    holo_count, rows, width = field_real.shape
    split = 2 if rows % 16 == 0 else 1
    block = rows // split
    field_spec = pl.BlockSpec((1, block, width), lambda k, j: (k, j, 0))
    return pl.pallas_call(
        encode_kernel,
        out_shape=jax.ShapeDtypeStruct((holo_count, 2, rows, width), jnp.float32),
        grid=(holo_count, split),
        in_specs=[
            pl.BlockSpec(memory_space=pltpu.SMEM),
            pl.BlockSpec((block, 1), lambda k, j: (j, 0)),
            field_spec,
            field_spec,
        ],
        out_specs=pl.BlockSpec((1, 2, block, width), lambda k, j: (k, 0, j, 0)),
    )(peak, parity, field_real, field_imag)


def solution(mesh):
    placed = (P(None, "row", "col"), P(), P())
    return jax.shard_map(
        body,
        mesh=mesh,
        in_specs=placed,
        out_specs=P(None, None, ("row", "col"), None),
        check_vma=False,
    )
```

```python
import math

import jax
import jax.numpy as jnp
from jax import lax
from jax.experimental import pallas as pl
from jax.experimental.pallas import tpu as pltpu
from jax.sharding import PartitionSpec as P

H = 8192
S = 2048
P_SIZE = 4096
MOST = 3


two_pi = 2.0 * math.pi
radix = 128
headroom = 1.25
softness = 0.01
epsilon = 1e-06


def contract(form, left, right):
    return jnp.einsum(
        form, left, right, precision=lax.Precision.HIGH, preferred_element_type=jnp.float32
    )


def make_tables(frequency, in_len, length, offset, sign):
    accum = length // radix
    blocks = in_len // radix
    first = frequency[:, :accum] % accum
    inner_index = first[:, :, None] * jnp.arange(blocks, dtype=jnp.int32)[None, None, :] % accum
    inner_angle = sign * two_pi / accum * inner_index.astype(jnp.float32)
    column = (jnp.arange(radix, dtype=jnp.int32) + offset) % length
    outer_index = frequency[:, :, None] * column[None, None, :] % length
    outer_angle = sign * two_pi / length * outer_index.astype(jnp.float32)
    shape_four = (frequency.shape[0], frequency.shape[1] // accum, accum, radix)
    return lax.optimization_barrier(
        (
            jnp.cos(inner_angle),
            jnp.sin(inner_angle),
            jnp.cos(outer_angle).reshape(shape_four),
            jnp.sin(outer_angle).reshape(shape_four),
        )
    )


def transform(real_part, imag_part, tables):
    inner_cos, inner_sin, outer_cos, outer_sin = tables
    batch, rows, width = real_part.shape
    blocks = width // radix
    real_four = real_part.reshape(batch, rows, blocks, radix)
    mid_real = contract("kpa,krab->krpb", inner_cos, real_four)
    mid_imag = contract("kpa,krab->krpb", inner_sin, real_four)
    if imag_part is not None:
        imag_four = imag_part.reshape(batch, rows, blocks, radix)
        mid_real = mid_real - contract("kpa,krab->krpb", inner_sin, imag_four)
        mid_imag = mid_imag + contract("kpa,krab->krpb", inner_cos, imag_four)
    return finish(mid_real, mid_imag, tables)


def finish(mid_real, mid_imag, tables):
    inner_cos, inner_sin, outer_cos, outer_sin = tables
    batch, rows = mid_real.shape[:2]
    out_real = contract("kqpb,krpb->krqp", outer_cos, mid_real) - contract(
        "kqpb,krpb->krqp", outer_sin, mid_imag
    )
    out_imag = contract("kqpb,krpb->krqp", outer_cos, mid_imag) + contract(
        "kqpb,krpb->krqp", outer_sin, mid_real
    )
    count = outer_cos.shape[1] * outer_cos.shape[2]
    return (out_real.reshape(batch, rows, count), out_imag.reshape(batch, rows, count))


def encode(field_real, field_imag, peak):
    scale = headroom * peak + epsilon
    unit_real = field_real / scale
    unit_imag = field_imag / scale
    square = unit_real * unit_real + unit_imag * unit_imag
    height = jnp.sqrt(1.0 - square)
    spread = jnp.sqrt(square + softness)
    phase_real = unit_real / spread
    phase_imag = unit_imag / spread
    plus_real = unit_real - phase_imag * height
    plus_imag = unit_imag + phase_real * height
    minus_real = unit_real + phase_imag * height
    minus_imag = unit_imag - phase_real * height
    return (plus_real, plus_imag, minus_real, minus_imag)


def body(holograms, sideband_centre, strip_owner):
    holo_count = holograms.shape[0]
    row_devices = lax.axis_size("row")
    col_devices = lax.axis_size("col")
    devices = row_devices * col_devices
    half = S // 2
    offsets = jnp.arange(S, dtype=jnp.int32) - half
    along_u = (sideband_centre[:, 0:1] + offsets[None, :]) % H
    along_v = (sideband_centre[:, 1:2] + offsets[None, :]) % H
    table_v = make_tables(along_v, H, H, 0, -1.0)
    table_u = make_tables(along_u, H, H, 0, -1.0)
    pixels = jnp.broadcast_to(jnp.arange(P_SIZE, dtype=jnp.int32)[None, :], (holo_count, P_SIZE))
    table_p = make_tables(pixels, S, P_SIZE, P_SIZE - half, 1.0)
    local_rows = holograms.shape[1]
    local_cols = holograms.shape[2]
    blocks = holograms.reshape(holo_count, col_devices, local_rows // col_devices, local_cols)
    piece = lax.all_to_all(blocks, "col", split_axis=1, concat_axis=1, tiled=True)
    lead, senders, count, width = piece.shape
    single = 1
    sender_blocks = width // radix
    piece_five = piece.reshape(lead, senders, count, sender_blocks, radix)
    inner_cos, inner_sin = table_v[0], table_v[1]
    per_sender = inner_cos.shape[:2] + (senders, sender_blocks)
    mid_real = contract("kpjc,kjrcb->krpb", inner_cos.reshape(per_sender), piece_five)
    mid_imag = contract("kpjc,kjrcb->krpb", inner_sin.reshape(per_sender), piece_five)
    share = S // devices
    outer_cos, outer_sin = table_v[2], table_v[3]
    form = "kqpb,krpb->qpkr"
    spec_real = contract(form, outer_cos, mid_real) - contract(form, outer_sin, mid_imag)
    spec_imag = contract(form, outer_cos, mid_imag) + contract(form, outer_sin, mid_real)
    send_shape = (devices, share, holo_count, count)
    piece_real = lax.all_to_all(spec_real.reshape(send_shape), ("row", "col"), 0, 0, tiled=True)
    piece_imag = lax.all_to_all(spec_imag.reshape(send_shape), ("row", "col"), 0, 0, tiled=True)
    pair = radix // count
    col_blocks = devices // pair
    recv_shape = (col_blocks, pair, share, holo_count, count)
    recv_real = piece_real.reshape(recv_shape)
    recv_imag = piece_imag.reshape(recv_shape)
    inner_cos, inner_sin = table_u[0], table_u[1]
    step = "kpa,alskr->ksplr"
    mid_real = contract(step, inner_cos, recv_real) - contract(step, inner_sin, recv_imag)
    mid_imag = contract(step, inner_sin, recv_real) + contract(step, inner_cos, recv_imag)
    mid_shape = (holo_count, share, inner_cos.shape[1], radix)
    side_real, side_imag = finish(mid_real.reshape(mid_shape), mid_imag.reshape(mid_shape), table_u)
    strips = strip_owner.shape[0]
    strip_rows = P_SIZE // strips
    slot_rows = MOST * strip_rows
    strip_ids = jnp.arange(strips, dtype=jnp.int32)
    same = strip_owner[:, None] == strip_owner[None, :]
    before = strip_ids[None, :] < strip_ids[:, None]
    rank = jnp.sum((same & before).astype(jnp.int32), axis=1)
    slot_of = strip_owner * MOST + rank
    slot_ids = jnp.arange(strips * MOST, dtype=jnp.int32)
    match = slot_of[None, :] == slot_ids[:, None]
    source = jnp.sum(jnp.where(match, strip_ids[None, :], 0), axis=1)
    filled = jnp.any(match, axis=1).astype(jnp.float32)

    inner_cos, inner_sin, outer_cos, outer_sin = table_p
    side_shape = (holo_count, share, S // radix, radix)
    side_real = side_real.reshape(side_shape)
    side_imag = side_imag.reshape(side_shape)
    step = "kpa,krab->krpb"
    mid_real = contract(step, inner_cos, side_real) - contract(step, inner_sin, side_imag)
    mid_imag = contract(step, inner_sin, side_real) + contract(step, inner_cos, side_imag)
    form = "kqpb,krpb->qkrp"
    lift_real = contract(form, outer_cos, mid_real) - contract(form, outer_sin, mid_imag)
    lift_imag = contract(form, outer_cos, mid_imag) + contract(form, outer_sin, mid_real)
    dense = (devices, 1, MOST * holo_count * share * strip_rows)

    def pack(part):
        grouped = part.reshape(strips, holo_count * share * strip_rows)
        picked = jnp.take(grouped, source, axis=0) * filled[:, None]
        return picked.reshape(dense)

    piece_real = lax.all_to_all(pack(lift_real), ("row", "col"), 0, 0, tiled=True)
    piece_imag = lax.all_to_all(pack(lift_imag), ("row", "col"), 0, 0, tiled=True)

    def unpack(piece):
        piece = piece.reshape(devices, MOST, holo_count, share, strip_rows)
        rows = jnp.transpose(piece, (2, 1, 4, 0, 3))
        return rows.reshape(holo_count, slot_rows, devices * share)

    rows_real = unpack(piece_real)
    rows_imag = unpack(piece_imag)
    out_real, out_imag = transform(rows_real, rows_imag, table_p)
    field_real = out_real.reshape(holo_count, slot_rows, P_SIZE)
    field_imag = out_imag.reshape(holo_count, slot_rows, P_SIZE)
    magnitude = jnp.sqrt(field_real * field_real + field_imag * field_imag)
    local_peak = jnp.max(magnitude, axis=(1, 2))
    every = jnp.broadcast_to(local_peak[None, :], (devices, holo_count))
    peak = jnp.max(lax.all_to_all(every, ("row", "col"), 0, 0, tiled=True), axis=0)
    device_index = lax.axis_index("row") * col_devices + lax.axis_index("col")
    my_source = lax.dynamic_slice_in_dim(source, device_index * MOST, MOST)
    row_number = (
        my_source[:, None] * strip_rows + jnp.arange(strip_rows, dtype=jnp.int32)[None, :]
    ).reshape(slot_rows)
    parity = (row_number % 2)[:, None]
    return encode_slots(peak, parity, field_real, field_imag)


def encode_kernel(peak_ref, parity_ref, real_ref, imag_ref, out_ref):
    inverse = 1.0 / (headroom * peak_ref[pl.program_id(0)] + epsilon)
    unit_real = real_ref[0] * inverse
    unit_imag = imag_ref[0] * inverse
    square = unit_real * unit_real + unit_imag * unit_imag
    height = jnp.sqrt(1.0 - square)
    shrink = lax.rsqrt(square + softness) * height
    phase_real = unit_real * shrink
    phase_imag = unit_imag * shrink
    plus_real = unit_real - phase_imag
    plus_imag = unit_imag + phase_real
    minus_real = unit_real + phase_imag
    minus_imag = unit_imag - phase_real
    column = lax.broadcasted_iota(jnp.int32, plus_real.shape, 1)
    even = (parity_ref[...] + column) % 2 == 0
    out_ref[0, 0] = jnp.where(even, plus_real, minus_real)
    out_ref[0, 1] = jnp.where(even, plus_imag, minus_imag)


def encode_slots(peak, parity, field_real, field_imag):
    holo_count, rows, width = field_real.shape
    split = 2 if rows % 16 == 0 else 1
    block = rows // split
    field_spec = pl.BlockSpec((1, block, width), lambda k, j: (k, j, 0))
    return pl.pallas_call(
        encode_kernel,
        out_shape=jax.ShapeDtypeStruct((holo_count, 2, rows, width), jnp.float32),
        grid=(holo_count, split),
        in_specs=[
            pl.BlockSpec(memory_space=pltpu.SMEM),
            pl.BlockSpec((block, 1), lambda k, j: (j, 0)),
            field_spec,
            field_spec,
        ],
        out_specs=pl.BlockSpec((1, 2, block, width), lambda k, j: (k, 0, j, 0)),
    )(peak, parity, field_real, field_imag)


def solution(mesh):
    placed = (P(None, "row", "col"), P(), P())
    return jax.shard_map(
        body,
        mesh=mesh,
        in_specs=placed,
        out_specs=P(None, None, ("row", "col"), None),
        check_vma=False,
    )
```

```python
import math

import jax
import jax.numpy as jnp
from jax import lax
from jax.experimental import pallas as pl
from jax.experimental.pallas import tpu as pltpu
from jax.sharding import PartitionSpec as P

H = 8192
S = 2048
P_SIZE = 4096
MOST = 3


two_pi = 2.0 * math.pi
radix = 128
headroom = 1.25
softness = 0.01
epsilon = 1e-06


def contract(form, left, right):
    return jnp.einsum(
        form, left, right, precision=lax.Precision.HIGH, preferred_element_type=jnp.float32
    )


def make_tables(frequency, in_len, length, offset, sign):
    accum = length // radix
    blocks = in_len // radix
    first = frequency[:, :accum] % accum
    inner_index = first[:, :, None] * jnp.arange(blocks, dtype=jnp.int32)[None, None, :] % accum
    inner_angle = sign * two_pi / accum * inner_index.astype(jnp.float32)
    column = (jnp.arange(radix, dtype=jnp.int32) + offset) % length
    outer_index = frequency[:, :, None] * column[None, None, :] % length
    outer_angle = sign * two_pi / length * outer_index.astype(jnp.float32)
    shape_four = (frequency.shape[0], frequency.shape[1] // accum, accum, radix)
    return lax.optimization_barrier(
        (
            jnp.cos(inner_angle),
            jnp.sin(inner_angle),
            jnp.cos(outer_angle).reshape(shape_four),
            jnp.sin(outer_angle).reshape(shape_four),
        )
    )


def transform(real_part, imag_part, tables):
    inner_cos, inner_sin, outer_cos, outer_sin = tables
    batch, rows, width = real_part.shape
    blocks = width // radix
    real_four = real_part.reshape(batch, rows, blocks, radix)
    mid_real = contract("kpa,krab->krpb", inner_cos, real_four)
    mid_imag = contract("kpa,krab->krpb", inner_sin, real_four)
    if imag_part is not None:
        imag_four = imag_part.reshape(batch, rows, blocks, radix)
        mid_real = mid_real - contract("kpa,krab->krpb", inner_sin, imag_four)
        mid_imag = mid_imag + contract("kpa,krab->krpb", inner_cos, imag_four)
    return finish(mid_real, mid_imag, tables)


def finish(mid_real, mid_imag, tables):
    inner_cos, inner_sin, outer_cos, outer_sin = tables
    batch, rows = mid_real.shape[:2]
    out_real = contract("kqpb,krpb->krqp", outer_cos, mid_real) - contract(
        "kqpb,krpb->krqp", outer_sin, mid_imag
    )
    out_imag = contract("kqpb,krpb->krqp", outer_cos, mid_imag) + contract(
        "kqpb,krpb->krqp", outer_sin, mid_real
    )
    count = outer_cos.shape[1] * outer_cos.shape[2]
    return (out_real.reshape(batch, rows, count), out_imag.reshape(batch, rows, count))


def encode(field_real, field_imag, peak):
    scale = headroom * peak + epsilon
    unit_real = field_real / scale
    unit_imag = field_imag / scale
    square = unit_real * unit_real + unit_imag * unit_imag
    height = jnp.sqrt(1.0 - square)
    spread = jnp.sqrt(square + softness)
    phase_real = unit_real / spread
    phase_imag = unit_imag / spread
    plus_real = unit_real - phase_imag * height
    plus_imag = unit_imag + phase_real * height
    minus_real = unit_real + phase_imag * height
    minus_imag = unit_imag - phase_real * height
    return (plus_real, plus_imag, minus_real, minus_imag)


def body(holograms, sideband_centre, strip_owner):
    holo_count = holograms.shape[0]
    row_devices = lax.axis_size("row")
    col_devices = lax.axis_size("col")
    devices = row_devices * col_devices
    half = S // 2
    offsets = jnp.arange(S, dtype=jnp.int32) - half
    along_u = (sideband_centre[:, 0:1] + offsets[None, :]) % H
    along_v = (sideband_centre[:, 1:2] + offsets[None, :]) % H
    table_v = make_tables(along_v, H, H, 0, -1.0)
    table_u = make_tables(along_u, H, H, 0, -1.0)
    pixels = jnp.broadcast_to(jnp.arange(P_SIZE, dtype=jnp.int32)[None, :], (holo_count, P_SIZE))
    table_p = make_tables(pixels, S, P_SIZE, P_SIZE - half, 1.0)
    local_rows = holograms.shape[1]
    local_cols = holograms.shape[2]
    blocks = holograms.reshape(holo_count, col_devices, local_rows // col_devices, local_cols)
    piece = lax.all_to_all(blocks, "col", split_axis=1, concat_axis=1, tiled=True)
    lead, senders, count, width = piece.shape
    single = 1
    sender_blocks = width // radix
    piece_five = piece.reshape(lead, senders, count, sender_blocks, radix)
    inner_cos, inner_sin = table_v[0], table_v[1]
    per_sender = inner_cos.shape[:2] + (senders, sender_blocks)
    mid_real = contract("kpjc,kjrcb->krpb", inner_cos.reshape(per_sender), piece_five)
    mid_imag = contract("kpjc,kjrcb->krpb", inner_sin.reshape(per_sender), piece_five)
    share = S // devices
    outer_cos, outer_sin = table_v[2], table_v[3]
    form = "kqpb,krpb->qpkr"
    spec_real = contract(form, outer_cos, mid_real) - contract(form, outer_sin, mid_imag)
    spec_imag = contract(form, outer_cos, mid_imag) + contract(form, outer_sin, mid_real)
    send_shape = (devices, share, holo_count, count)
    piece_real = lax.all_to_all(spec_real.reshape(send_shape), ("row", "col"), 0, 0, tiled=True)
    piece_imag = lax.all_to_all(spec_imag.reshape(send_shape), ("row", "col"), 0, 0, tiled=True)
    pair = radix // count
    col_blocks = devices // pair
    recv_shape = (col_blocks, pair, share, holo_count, count)
    recv_real = piece_real.reshape(recv_shape)
    recv_imag = piece_imag.reshape(recv_shape)
    inner_cos, inner_sin = table_u[0], table_u[1]
    step = "kpa,alskr->ksplr"
    mid_real = contract(step, inner_cos, recv_real) - contract(step, inner_sin, recv_imag)
    mid_imag = contract(step, inner_sin, recv_real) + contract(step, inner_cos, recv_imag)
    mid_shape = (holo_count, share, inner_cos.shape[1], radix)
    side_real, side_imag = finish(mid_real.reshape(mid_shape), mid_imag.reshape(mid_shape), table_u)
    lift_real, lift_imag = transform(
        side_real.reshape(holo_count, share, S), side_imag.reshape(holo_count, share, S), table_p
    )
    strips = strip_owner.shape[0]
    strip_rows = P_SIZE // strips
    slot_rows = MOST * strip_rows
    strip_ids = jnp.arange(strips, dtype=jnp.int32)
    same = strip_owner[:, None] == strip_owner[None, :]
    before = strip_ids[None, :] < strip_ids[:, None]
    rank = jnp.sum((same & before).astype(jnp.int32), axis=1)
    slot_of = strip_owner * MOST + rank
    slot_ids = jnp.arange(strips * MOST, dtype=jnp.int32)
    match = slot_of[None, :] == slot_ids[:, None]
    source = jnp.sum(jnp.where(match, strip_ids[None, :], 0), axis=1)
    filled = jnp.any(match, axis=1).astype(jnp.float32)

    def pack(part):
        grouped = part.reshape(holo_count, share, strips, strip_rows)
        picked = jnp.take(grouped, source, axis=2) * filled[None, None, :, None]
        return jnp.transpose(picked.reshape(holo_count, share, strips, slot_rows), (2, 0, 1, 3))

    send_real = pack(lift_real)
    send_imag = pack(lift_imag)
    dense = (devices, 1, holo_count * share * slot_rows)
    piece_real = lax.all_to_all(send_real.reshape(dense), ("row", "col"), 0, 0, tiled=True)
    piece_imag = lax.all_to_all(send_imag.reshape(dense), ("row", "col"), 0, 0, tiled=True)

    def unpack(piece):
        piece = piece.reshape(devices, holo_count, share, slot_rows)
        return jnp.transpose(piece, (1, 3, 0, 2)).reshape(holo_count, slot_rows, devices * share)

    rows_real = unpack(piece_real)
    rows_imag = unpack(piece_imag)
    out_real, out_imag = transform(rows_real, rows_imag, table_p)
    field_real = out_real.reshape(holo_count, slot_rows, P_SIZE)
    field_imag = out_imag.reshape(holo_count, slot_rows, P_SIZE)
    magnitude = jnp.sqrt(field_real * field_real + field_imag * field_imag)
    local_peak = jnp.max(magnitude, axis=(1, 2))
    every = jnp.broadcast_to(local_peak[None, :], (devices, holo_count))
    peak = jnp.max(lax.all_to_all(every, ("row", "col"), 0, 0, tiled=True), axis=0)
    device_index = lax.axis_index("row") * col_devices + lax.axis_index("col")
    my_source = lax.dynamic_slice_in_dim(source, device_index * MOST, MOST)
    row_number = (
        my_source[:, None] * strip_rows + jnp.arange(strip_rows, dtype=jnp.int32)[None, :]
    ).reshape(slot_rows)
    parity = (row_number % 2)[:, None]
    return encode_slots(peak, parity, field_real, field_imag)


def encode_kernel(peak_ref, parity_ref, real_ref, imag_ref, out_ref):
    inverse = 1.0 / (headroom * peak_ref[pl.program_id(0)] + epsilon)
    unit_real = real_ref[0] * inverse
    unit_imag = imag_ref[0] * inverse
    square = unit_real * unit_real + unit_imag * unit_imag
    height = jnp.sqrt(1.0 - square)
    shrink = lax.rsqrt(square + softness) * height
    phase_real = unit_real * shrink
    phase_imag = unit_imag * shrink
    plus_real = unit_real - phase_imag
    plus_imag = unit_imag + phase_real
    minus_real = unit_real + phase_imag
    minus_imag = unit_imag - phase_real
    column = lax.broadcasted_iota(jnp.int32, plus_real.shape, 1)
    even = (parity_ref[...] + column) % 2 == 0
    out_ref[0, 0] = jnp.where(even, plus_real, minus_real)
    out_ref[0, 1] = jnp.where(even, plus_imag, minus_imag)


def encode_slots(peak, parity, field_real, field_imag):
    holo_count, rows, width = field_real.shape
    split = 4 if rows % 32 == 0 else 1
    block = rows // split
    field_spec = pl.BlockSpec((1, block, width), lambda k, j: (k, j, 0))
    return pl.pallas_call(
        encode_kernel,
        out_shape=jax.ShapeDtypeStruct((holo_count, 2, rows, width), jnp.float32),
        grid=(holo_count, split),
        in_specs=[
            pl.BlockSpec(memory_space=pltpu.SMEM),
            pl.BlockSpec((block, 1), lambda k, j: (j, 0)),
            field_spec,
            field_spec,
        ],
        out_specs=pl.BlockSpec((1, 2, block, width), lambda k, j: (k, 0, j, 0)),
    )(peak, parity, field_real, field_imag)


def solution(mesh):
    placed = (P(None, "row", "col"), P(), P())
    return jax.shard_map(
        body,
        mesh=mesh,
        in_specs=placed,
        out_specs=P(None, None, ("row", "col"), None),
        check_vma=False,
    )
```
